32 devices in a mesh: dp: 4 (over z), tensor: 8 (over y, x, core).
Axes of the slice: x: 2, y: 2, z: 4, core: 2. Of those that a mesh axis runs over, the one named last changes fastest.
Arguments:
- inputs: bfloat16 [4, 32, 4096], P(None, 'tensor', 'dp'), may hold values from -6 to 6
- norm_gain: float32 [4096], P('dp'), may hold values from 0.1 to 1.9
- w_gate: bfloat16 [4096, 28672], P('dp', 'tensor'), may hold values from -0.09375 to 0.09375
- w_up: bfloat16 [4096, 28672], P('dp', 'tensor'), may hold values from -0.09375 to 0.09375
- w_down: bfloat16 [28672, 4096], P('tensor', 'dp'), may hold values from -0.03125 to 0.03125
- d_output: bfloat16 [4, 32, 4096], P(None, 'tensor', 'dp'), may hold values from -0.75 to 0.75
- level_of_batch: int32 [4], replicated, may hold values from 0 to 3, each once
Outputs:
- outputs: bfloat16 [4, 32, 4096], P(None, 'tensor', 'dp')
- d_inputs: bfloat16 [4, 32, 4096], P(None, 'tensor', 'dp')
- d_gain: float32 [4096], P('dp')
- d_gate: bfloat16 [4096, 28672], P('dp', 'tensor')
- d_up: bfloat16 [4096, 28672], P('dp', 'tensor')
- d_down: bfloat16 [28672, 4096], P('tensor', 'dp')
- row_product: float32 [4, 32], P(None, 'tensor')
The draws below stay inside these ranges and needn't reach their ends.
Inputs may be any that keep to these rules, and one draw needn't show every extreme that they name: `level_of_batch`: every level from 0 to 3 belongs to exactly one micro-batch.
All inputs are finite; a program needn't handle non-finite values.
Results may differ from the reference program's by a relative error of at most 0.02.
Values may be sent and summed in bfloat16 or wider, within the bound.
No kernel may reach another device: no remote copies, remote signals or barrier semaphores. Data moves between devices by JAX's collectives and lax.ppermute only.
A program may use at most 384 MiB of HBM per device.

```python
import jax
import jax.numpy as jnp
from jax import lax

D = 4096
FF = 28672
MB = 4
ROWS = 32
N_DP = 4


def levels(rng, shape, shards, low, high):
    loudness, own = 1.0, jax.random.fold_in(rng, 6)
    for position, shards_of in shards:
        heights = jnp.exp(jax.random.uniform(jax.random.fold_in(own, position), (shards_of,), jnp.float32, low / len(shards), high / len(shards)))
        loudness = loudness * jnp.repeat(heights, shape[position] // shards_of).reshape([-1 if axis == position else 1 for axis in range(len(shape))])
    return loudness


def noise(stream_key, extent, deviation, most, cuts=(), kind=jnp.bfloat16):
    factor_of = levels(stream_key, extent, cuts, -0.22, 0.18) if cuts else 1.0
    entries = jax.random.normal(stream_key, extent, jnp.float32) * deviation * factor_of
    return jnp.minimum(jnp.maximum(entries, -most), most).astype(kind)


def setup_inputs(seed: int = 0) -> dict:
    streams_of = jax.random.split(jax.random.key(seed), 8)
    return {
        "inputs": noise(streams_of[0], (MB, ROWS, D), 1.0, 6.0, ((1, 8), (2, 4))),
        "norm_gain": jnp.clip(1.0 + 0.18 * jax.random.normal(streams_of[1], (D,), jnp.float32), 0.1, 1.9),
        "w_gate": noise(streams_of[2], (D, FF), D ** -0.5, 0.09375, ((0, 4), (1, 8))),
        "w_up": noise(streams_of[3], (D, FF), D ** -0.5, 0.09375, ((0, 4), (1, 8))),
        "w_down": noise(streams_of[4], (FF, D), FF ** -0.5, 0.03125, ((0, 8), (1, 4))),
        "d_output": noise(streams_of[5], (MB, ROWS, D), 0.125, 0.75, ((1, 8), (2, 4))),
        "level_of_batch": jax.random.permutation(streams_of[6], MB).astype(jnp.int32),
    }


epsilon = 1e-05

def split_sum(left_rows, right_cols):
    row_count = left_rows.shape[0]
    left_blocks = left_rows.astype(jnp.float32).reshape(row_count, N_DP, -1)
    right_blocks = right_cols.astype(jnp.float32).reshape(N_DP, -1, right_cols.shape[1])
    partial_terms = jnp.einsum('rid,idp->rip', left_blocks, right_blocks)
    rounded = lax.optimization_barrier(partial_terms.astype(jnp.bfloat16))
    return lax.optimization_barrier(jnp.sum(rounded.astype(jnp.float32), axis=1))

def reference(inputs, norm_gain, w_gate, w_up, w_down, d_output, level_of_batch):
    wide_inputs = inputs.astype(jnp.float32)
    full_width = wide_inputs.shape[2]
    row_scale = lax.rsqrt(lax.optimization_barrier(jnp.sum(wide_inputs * wide_inputs, axis=2)) / full_width + epsilon)
    normed = (wide_inputs * row_scale[:, :, None] * norm_gain).astype(jnp.bfloat16)
    positions = jnp.arange(MB, dtype=jnp.int32)
    gate_total = jnp.zeros((D, FF), jnp.float32)
    up_total = jnp.zeros((D, FF), jnp.float32)
    down_total = jnp.zeros((FF, D), jnp.float32)
    down_output = jnp.zeros(wide_inputs.shape, jnp.float32)
    normed_grad = jnp.zeros(wide_inputs.shape, jnp.float32)
    for prefix_level in range(4):
        columns_used = FF // 2 ** (3 - prefix_level)
        chosen = jnp.sum(jnp.where(level_of_batch == prefix_level, positions, 0)).astype(jnp.int32)
        normed_rows = lax.dynamic_index_in_dim(normed, chosen, 0, keepdims=False)
        grad_rows = lax.dynamic_index_in_dim(d_output, chosen, 0, keepdims=False)
        gate_view = w_gate[:, :columns_used]
        up_view = w_up[:, :columns_used]
        down_view = w_down[:columns_used]
        gate_sum = split_sum(normed_rows, gate_view)
        up_sum = split_sum(normed_rows, up_view)
        back_sum = split_sum(grad_rows, down_view.T)
        sigmoid_gate = jax.nn.sigmoid(gate_sum)
        silu_gate = gate_sum * sigmoid_gate
        slope = sigmoid_gate * (1.0 + gate_sum * (1.0 - sigmoid_gate))
        hidden = (silu_gate * up_sum).astype(jnp.bfloat16)
        gate_grad = (back_sum * up_sum * slope).astype(jnp.bfloat16)
        up_grad = (back_sum * silu_gate).astype(jnp.bfloat16)
        down_share = jnp.dot(hidden, down_view, preferred_element_type=jnp.float32)
        normed_share = jnp.dot(gate_grad, gate_view.T, preferred_element_type=jnp.float32) + jnp.dot(up_grad, up_view.T, preferred_element_type=jnp.float32)
        down_output = lax.dynamic_update_index_in_dim(down_output, down_share, chosen, 0)
        normed_grad = lax.dynamic_update_index_in_dim(normed_grad, normed_share, chosen, 0)
        down_total = down_total.at[:columns_used].add(jnp.dot(hidden.T, grad_rows, preferred_element_type=jnp.float32))
        gate_total = gate_total.at[:, :columns_used].add(jnp.dot(normed_rows.T, gate_grad, preferred_element_type=jnp.float32))
        up_total = up_total.at[:, :columns_used].add(jnp.dot(normed_rows.T, up_grad, preferred_element_type=jnp.float32))
    wide_grad = d_output.astype(jnp.float32)
    weighted = norm_gain * normed_grad
    row_product = lax.optimization_barrier(jnp.sum(weighted * wide_inputs, axis=2))
    d_gain = lax.optimization_barrier(jnp.sum(normed_grad * wide_inputs * row_scale[:, :, None], axis=(0, 1)))
    outputs = (wide_inputs + down_output).astype(jnp.bfloat16)
    scale_cube = row_scale * row_scale * row_scale
    d_inputs = (wide_grad + row_scale[:, :, None] * weighted - wide_inputs * (scale_cube * row_product / full_width)[:, :, None]).astype(jnp.bfloat16)
    return (outputs, d_inputs, d_gain, gate_total.astype(jnp.bfloat16), up_total.astype(jnp.bfloat16), down_total.astype(jnp.bfloat16), row_product)
```

```python
import jax
import jax.numpy as jnp
from jax import lax
from jax.sharding import PartitionSpec as P

epsilon = 1e-05
contract_cols = (((1,), (1,)), ((), ()))
contract_rows = (((0,), (0,)), ((), ()))


def local_terms(gate_sum, up_sum, back_sum, active_mask):
    sigmoid_gate = jax.nn.sigmoid(gate_sum)
    silu_gate = gate_sum * sigmoid_gate
    slope = sigmoid_gate * (1.0 + gate_sum * (1.0 - sigmoid_gate))
    hidden = (silu_gate * up_sum * active_mask).astype(jnp.bfloat16)
    gate_grad = (back_sum * up_sum * slope * active_mask).astype(jnp.bfloat16)
    up_grad = (back_sum * silu_gate * active_mask).astype(jnp.bfloat16)
    return (hidden, gate_grad, up_grad)


def per_device(inputs, norm_gain, w_gate, w_up, w_down, d_output, level_of_batch):
    groups = lax.axis_size("tensor")
    tensor_index = lax.axis_index("tensor")
    local_feat = w_gate.shape[0]
    local_cols = w_gate.shape[1]
    full_width = local_feat * lax.axis_size("dp")
    batches, local_rows, _ = inputs.shape
    both = jnp.concatenate([inputs, d_output], axis=0)
    both_all = lax.all_gather(both, "tensor", axis=1, tiled=True)
    inputs_all = both_all[:batches].astype(jnp.float32)
    grad_all = both_all[batches:]
    rows = inputs_all.shape[1]
    square_sum = lax.psum(jnp.sum(inputs_all * inputs_all, axis=2), "dp")
    row_scale_all = lax.rsqrt(square_sum / full_width + epsilon)
    normed_all = (inputs_all * row_scale_all[:, :, None] * norm_gain).astype(jnp.bfloat16)
    start = tensor_index * local_rows
    row_scale = lax.dynamic_slice_in_dim(row_scale_all, start, local_rows, axis=1)
    wide_inputs = inputs.astype(jnp.float32)

    flat_normed = normed_all.reshape(batches * rows, local_feat)
    flat_grad = grad_all.reshape(batches * rows, local_feat)
    gate_part = jnp.dot(flat_normed, w_gate, preferred_element_type=jnp.float32)
    up_part = jnp.dot(flat_normed, w_up, preferred_element_type=jnp.float32)
    back_part = lax.dot_general(
        flat_grad, w_down, contract_cols, preferred_element_type=jnp.float32
    )
    gate_sum, up_sum, back_sum = (
        lax.psum(gate_part.astype(jnp.bfloat16), "dp").astype(jnp.float32),
        lax.psum(up_part.astype(jnp.bfloat16), "dp").astype(jnp.float32),
        lax.psum(back_part.astype(jnp.bfloat16), "dp").astype(jnp.float32),
    )
    halvings = 3 - level_of_batch
    active = (tensor_index < jnp.right_shift(groups, halvings)).astype(jnp.float32)
    active_mask = jnp.repeat(active, rows)[:, None]
    hidden, gate_grad, up_grad = local_terms(gate_sum, up_sum, back_sum, active_mask)

    down_part = jnp.dot(hidden, w_down, preferred_element_type=jnp.float32)
    normed_part = lax.dot_general(
        gate_grad, w_gate, contract_cols, preferred_element_type=jnp.float32
    ) + lax.dot_general(up_grad, w_up, contract_cols, preferred_element_type=jnp.float32)
    stacked = jnp.stack([down_part, normed_part]).astype(jnp.bfloat16)
    stacked = stacked.reshape(2, batches, rows, local_feat)
    shares = lax.psum_scatter(stacked, "tensor", scatter_dimension=2, tiled=True).astype(
        jnp.float32
    )
    down_output = shares[0]
    normed_grad = shares[1]

    down_out = lax.dot_general(
        hidden, flat_grad, contract_rows, preferred_element_type=jnp.float32
    ).astype(jnp.bfloat16)
    gate_out = lax.dot_general(
        flat_normed, gate_grad, contract_rows, preferred_element_type=jnp.float32
    ).astype(jnp.bfloat16)
    up_out = lax.dot_general(
        flat_normed, up_grad, contract_rows, preferred_element_type=jnp.float32
    ).astype(jnp.bfloat16)

    wide_grad = d_output.astype(jnp.float32)
    weighted = norm_gain * normed_grad
    row_part = jnp.sum(weighted * wide_inputs, axis=2)
    gain_part = jnp.sum(normed_grad * wide_inputs * row_scale[:, :, None], axis=(0, 1))
    row_product = lax.psum(row_part, "dp")
    d_gain = lax.psum(gain_part, "tensor")
    outputs = (wide_inputs + down_output).astype(jnp.bfloat16)
    scale_cube = row_scale * row_scale * row_scale
    d_inputs = (
        wide_grad
        + row_scale[:, :, None] * weighted
        - wide_inputs * (scale_cube * row_product / full_width)[:, :, None]
    ).astype(jnp.bfloat16)
    return (outputs, d_inputs, d_gain, gate_out, up_out, down_out, row_product)


def solution(mesh):
    in_specs = (
        P(None, "tensor", "dp"),
        P("dp"),
        P("dp", "tensor"),
        P("dp", "tensor"),
        P("tensor", "dp"),
        P(None, "tensor", "dp"),
        P(),
    )
    out_specs = (
        P(None, "tensor", "dp"),
        P(None, "tensor", "dp"),
        P("dp"),
        P("dp", "tensor"),
        P("dp", "tensor"),
        P("tensor", "dp"),
        P(None, "tensor"),
    )
    return jax.shard_map(
        per_device, mesh=mesh, in_specs=in_specs, out_specs=out_specs, check_vma=False
    )
```

```python
import jax
import jax.numpy as jnp
from jax import lax
from jax.sharding import PartitionSpec as P

epsilon = 1e-05
contract_cols = (((1,), (1,)), ((), ()))
contract_rows = (((0,), (0,)), ((), ()))


def local_terms(gate_sum, up_sum, back_sum, active_mask):
    sigmoid_gate = jax.nn.sigmoid(gate_sum)
    silu_gate = gate_sum * sigmoid_gate
    slope = sigmoid_gate * (1.0 + gate_sum * (1.0 - sigmoid_gate))
    hidden = (silu_gate * up_sum * active_mask).astype(jnp.bfloat16)
    gate_grad = (back_sum * up_sum * slope * active_mask).astype(jnp.bfloat16)
    up_grad = (back_sum * silu_gate * active_mask).astype(jnp.bfloat16)
    return (hidden, gate_grad, up_grad)


def per_device(inputs, norm_gain, w_gate, w_up, w_down, d_output, level_of_batch):
    groups = lax.axis_size("tensor")
    tensor_index = lax.axis_index("tensor")
    local_feat = w_gate.shape[0]
    local_cols = w_gate.shape[1]
    full_width = local_feat * lax.axis_size("dp")
    batches, local_rows, _ = inputs.shape
    both = jnp.concatenate([inputs, d_output], axis=0).transpose(1, 0, 2)
    both_all = lax.all_gather(both, "tensor", axis=0, tiled=True)
    inputs_all = both_all[:, :batches].astype(jnp.float32)
    grad_all = both_all[:, batches:]
    rows = inputs_all.shape[0]
    square_sum = lax.psum(jnp.sum(inputs_all * inputs_all, axis=2), "dp")
    row_scale_all = lax.rsqrt(square_sum / full_width + epsilon)
    normed_all = (inputs_all * row_scale_all[:, :, None] * norm_gain).astype(jnp.bfloat16)
    start = tensor_index * local_rows
    row_scale = lax.dynamic_slice_in_dim(row_scale_all, start, local_rows, axis=0).T
    wide_inputs = inputs.astype(jnp.float32)

    flat_normed = normed_all.reshape(rows * batches, local_feat)
    flat_grad = grad_all.reshape(rows * batches, local_feat)
    gate_part = jnp.dot(flat_normed, w_gate, preferred_element_type=jnp.float32)
    up_part = jnp.dot(flat_normed, w_up, preferred_element_type=jnp.float32)
    back_part = lax.dot_general(
        flat_grad, w_down, contract_cols, preferred_element_type=jnp.float32
    )
    gate_sum, up_sum, back_sum = (
        lax.psum(gate_part.astype(jnp.bfloat16), "dp").astype(jnp.float32),
        lax.psum(up_part.astype(jnp.bfloat16), "dp").astype(jnp.float32),
        lax.psum(back_part.astype(jnp.bfloat16), "dp").astype(jnp.float32),
    )
    halvings = 3 - level_of_batch
    active = (tensor_index < jnp.right_shift(groups, halvings)).astype(jnp.float32)
    active_mask = jnp.tile(active, rows)[:, None]
    hidden, gate_grad, up_grad = local_terms(gate_sum, up_sum, back_sum, active_mask)

    down_part = jnp.dot(hidden, w_down, preferred_element_type=jnp.float32)
    normed_part = lax.dot_general(
        gate_grad, w_gate, contract_cols, preferred_element_type=jnp.float32
    ) + lax.dot_general(up_grad, w_up, contract_cols, preferred_element_type=jnp.float32)
    stacked = jnp.stack(
        [
            down_part.reshape(rows, batches, local_feat),
            normed_part.reshape(rows, batches, local_feat),
        ],
        axis=1,
    ).astype(jnp.bfloat16)
    stacked = stacked.reshape(rows, 2 * batches, local_feat)
    shares = lax.psum_scatter(stacked, "tensor", scatter_dimension=0, tiled=True).astype(
        jnp.float32
    )
    shares = shares.reshape(local_rows, 2, batches, local_feat)
    down_output = shares[:, 0].transpose(1, 0, 2)
    normed_grad = shares[:, 1].transpose(1, 0, 2)

    down_out = lax.dot_general(
        hidden, flat_grad, contract_rows, preferred_element_type=jnp.float32
    ).astype(jnp.bfloat16)
    gate_out = lax.dot_general(
        flat_normed, gate_grad, contract_rows, preferred_element_type=jnp.float32
    ).astype(jnp.bfloat16)
    up_out = lax.dot_general(
        flat_normed, up_grad, contract_rows, preferred_element_type=jnp.float32
    ).astype(jnp.bfloat16)

    wide_grad = d_output.astype(jnp.float32)
    weighted = norm_gain * normed_grad
    row_part = jnp.sum(weighted * wide_inputs, axis=2)
    gain_part = jnp.sum(normed_grad * wide_inputs * row_scale[:, :, None], axis=(0, 1))
    dp_index = lax.axis_index("dp")
    row_slots = jnp.zeros((groups,) + row_part.shape, jnp.float32)
    row_slots = lax.dynamic_update_index_in_dim(row_slots, row_part, tensor_index, 0)
    gain_slots = jnp.zeros((lax.axis_size("dp"), local_feat), jnp.float32)
    gain_slots = lax.dynamic_update_index_in_dim(gain_slots, gain_part, dp_index, 0)
    row_slots, gain_slots = lax.psum((row_slots, gain_slots), ("dp", "tensor"))
    row_product = lax.dynamic_index_in_dim(row_slots, tensor_index, 0, keepdims=False)
    d_gain = lax.dynamic_index_in_dim(gain_slots, dp_index, 0, keepdims=False)
    outputs = (wide_inputs + down_output).astype(jnp.bfloat16)
    scale_cube = row_scale * row_scale * row_scale
    d_inputs = (
        wide_grad
        + row_scale[:, :, None] * weighted
        - wide_inputs * (scale_cube * row_product / full_width)[:, :, None]
    ).astype(jnp.bfloat16)
    return (outputs, d_inputs, d_gain, gate_out, up_out, down_out, row_product)


def solution(mesh):
    in_specs = (
        P(None, "tensor", "dp"),
        P("dp"),
        P("dp", "tensor"),
        P("dp", "tensor"),
        P("tensor", "dp"),
        P(None, "tensor", "dp"),
        P(),
    )
    out_specs = (
        P(None, "tensor", "dp"),
        P(None, "tensor", "dp"),
        P("dp"),
        P("dp", "tensor"),
        P("dp", "tensor"),
        P("tensor", "dp"),
        P(None, "tensor"),
    )
    return jax.shard_map(
        per_device, mesh=mesh, in_specs=in_specs, out_specs=out_specs, check_vma=False
    )
```

```python
import jax
import jax.numpy as jnp
from jax import lax
from jax.sharding import PartitionSpec as P

epsilon = 1e-05
contract_cols = (((1,), (1,)), ((), ()))
contract_rows = (((0,), (0,)), ((), ()))


def local_terms(gate_sum, up_sum, back_sum, active_mask):
    sigmoid_gate = jax.nn.sigmoid(gate_sum)
    silu_gate = gate_sum * sigmoid_gate
    slope = sigmoid_gate * (1.0 + gate_sum * (1.0 - sigmoid_gate))
    hidden = (silu_gate * up_sum * active_mask).astype(jnp.bfloat16)
    gate_grad = (back_sum * up_sum * slope * active_mask).astype(jnp.bfloat16)
    up_grad = (back_sum * silu_gate * active_mask).astype(jnp.bfloat16)
    return (hidden, gate_grad, up_grad)


def per_device(inputs, norm_gain, w_gate, w_up, w_down, d_output, level_of_batch):
    groups = lax.axis_size("tensor")
    tensor_index = lax.axis_index("tensor")
    local_feat = w_gate.shape[0]
    local_cols = w_gate.shape[1]
    full_width = local_feat * lax.axis_size("dp")
    batches, local_rows, _ = inputs.shape
    both = jnp.concatenate([inputs, d_output], axis=0).transpose(1, 0, 2)
    both_all = lax.all_gather(both, "tensor", axis=0, tiled=True)
    inputs_all = both_all[:, :batches].astype(jnp.float32)
    grad_all = both_all[:, batches:]
    rows = inputs_all.shape[0]
    square_sum = lax.psum(jnp.sum(inputs_all * inputs_all, axis=2).T, "dp").T
    row_scale_all = lax.rsqrt(square_sum / full_width + epsilon)
    normed_all = (inputs_all * row_scale_all[:, :, None] * norm_gain).astype(jnp.bfloat16)
    start = tensor_index * local_rows
    row_scale = lax.dynamic_slice_in_dim(row_scale_all, start, local_rows, axis=0).T
    wide_inputs = inputs.astype(jnp.float32)

    flat_normed = normed_all.reshape(rows * batches, local_feat)
    flat_grad = grad_all.reshape(rows * batches, local_feat)
    halvings = 3 - level_of_batch
    active = (tensor_index < jnp.right_shift(groups, halvings)).astype(jnp.float32)
    active_mask = jnp.tile(active, rows)[:, None]
    chunks = 2
    width = local_cols // chunks
    down_part = None
    normed_part = None
    hiddens, gate_grads, up_grads = [], [], []
    previous = None
    for chunk in range(chunks):
        cols = slice(chunk * width, (chunk + 1) * width)
        gate_w = w_gate[:, cols]
        up_w = w_up[:, cols]
        down_w = w_down[cols, :]
        gate_part = jnp.dot(flat_normed, gate_w, preferred_element_type=jnp.float32)
        up_part = jnp.dot(flat_normed, up_w, preferred_element_type=jnp.float32)
        back_part = lax.dot_general(
            flat_grad, down_w, contract_cols, preferred_element_type=jnp.float32
        )
        parts = (
            gate_part.astype(jnp.bfloat16),
            up_part.astype(jnp.bfloat16),
            back_part.astype(jnp.bfloat16),
        )
        if previous is not None:
            parts, _ = lax.optimization_barrier((parts, previous))
        gate_sum, up_sum, back_sum = lax.psum(parts, "dp")
        previous = (gate_sum, up_sum, back_sum)
        hidden, gate_grad, up_grad = local_terms(
            gate_sum.astype(jnp.float32),
            up_sum.astype(jnp.float32),
            back_sum.astype(jnp.float32),
            active_mask,
        )
        hiddens.append(hidden)
        gate_grads.append(gate_grad)
        up_grads.append(up_grad)
        down_term = jnp.dot(hidden, down_w, preferred_element_type=jnp.float32)
        normed_term = lax.dot_general(
            gate_grad, gate_w, contract_cols, preferred_element_type=jnp.float32
        ) + lax.dot_general(up_grad, up_w, contract_cols, preferred_element_type=jnp.float32)
        down_part = down_term if down_part is None else down_part + down_term
        normed_part = normed_term if normed_part is None else normed_part + normed_term
    hidden = jnp.concatenate(hiddens, axis=1)
    gate_grad = jnp.concatenate(gate_grads, axis=1)
    up_grad = jnp.concatenate(up_grads, axis=1)

    stacked = jnp.stack(
        [
            down_part.reshape(rows, batches, local_feat),
            normed_part.reshape(rows, batches, local_feat),
        ],
        axis=1,
    ).astype(jnp.bfloat16)
    stacked = stacked.reshape(rows, 2 * batches, local_feat)
    shares = lax.psum_scatter(stacked, "tensor", scatter_dimension=0, tiled=True).astype(
        jnp.float32
    )
    shares = shares.reshape(local_rows, 2, batches, local_feat)
    down_output = shares[:, 0].transpose(1, 0, 2)
    normed_grad = shares[:, 1].transpose(1, 0, 2)

    down_out = lax.dot_general(
        hidden, flat_grad, contract_rows, preferred_element_type=jnp.float32
    ).astype(jnp.bfloat16)
    gate_out = lax.dot_general(
        flat_normed, gate_grad, contract_rows, preferred_element_type=jnp.float32
    ).astype(jnp.bfloat16)
    up_out = lax.dot_general(
        flat_normed, up_grad, contract_rows, preferred_element_type=jnp.float32
    ).astype(jnp.bfloat16)

    wide_grad = d_output.astype(jnp.float32)
    weighted = norm_gain * normed_grad
    row_part = jnp.sum(weighted * wide_inputs, axis=2)
    gain_part = jnp.sum(normed_grad * wide_inputs * row_scale[:, :, None], axis=(0, 1))
    row_product = lax.psum(row_part, "dp")
    d_gain = lax.psum(gain_part, "tensor")
    outputs = (wide_inputs + down_output).astype(jnp.bfloat16)
    scale_cube = row_scale * row_scale * row_scale
    d_inputs = (
        wide_grad
        + row_scale[:, :, None] * weighted
        - wide_inputs * (scale_cube * row_product / full_width)[:, :, None]
    ).astype(jnp.bfloat16)
    return (outputs, d_inputs, d_gain, gate_out, up_out, down_out, row_product)


def solution(mesh):
    in_specs = (
        P(None, "tensor", "dp"),
        P("dp"),
        P("dp", "tensor"),
        P("dp", "tensor"),
        P("tensor", "dp"),
        P(None, "tensor", "dp"),
        P(),
    )
    out_specs = (
        P(None, "tensor", "dp"),
        P(None, "tensor", "dp"),
        P("dp"),
        P("dp", "tensor"),
        P("dp", "tensor"),
        P("tensor", "dp"),
        P(None, "tensor"),
    )
    return jax.shard_map(
        per_device, mesh=mesh, in_specs=in_specs, out_specs=out_specs, check_vma=False
    )
```

```python
import jax
import jax.numpy as jnp
from jax import lax
from jax.sharding import PartitionSpec as P

epsilon = 1e-05
contract_cols = (((1,), (1,)), ((), ()))
contract_rows = (((0,), (0,)), ((), ()))


def local_terms(gate_sum, up_sum, back_sum, active_mask):
    sigmoid_gate = jax.nn.sigmoid(gate_sum)
    silu_gate = gate_sum * sigmoid_gate
    slope = sigmoid_gate * (1.0 + gate_sum * (1.0 - sigmoid_gate))
    hidden = (silu_gate * up_sum * active_mask).astype(jnp.bfloat16)
    gate_grad = (back_sum * up_sum * slope * active_mask).astype(jnp.bfloat16)
    up_grad = (back_sum * silu_gate * active_mask).astype(jnp.bfloat16)
    return (hidden, gate_grad, up_grad)


def per_device(inputs, norm_gain, w_gate, w_up, w_down, d_output, level_of_batch):
    groups = lax.axis_size("tensor")
    tensor_index = lax.axis_index("tensor")
    local_feat = w_gate.shape[0]
    local_cols = w_gate.shape[1]
    full_width = local_feat * lax.axis_size("dp")
    batches, local_rows, _ = inputs.shape
    wide_inputs = inputs.astype(jnp.float32)
    square_sum = lax.psum(jnp.sum(wide_inputs * wide_inputs, axis=2), "dp")
    row_scale = lax.rsqrt(square_sum / full_width + epsilon)
    normed = (wide_inputs * row_scale[:, :, None] * norm_gain).astype(jnp.bfloat16)
    both = jnp.concatenate([normed, d_output], axis=0).transpose(1, 0, 2)
    both_all = lax.all_gather(both, "tensor", axis=0, tiled=True)
    normed_all = both_all[:, :batches]
    grad_all = both_all[:, batches:]
    rows = normed_all.shape[0]

    flat_normed = normed_all.reshape(rows * batches, local_feat)
    flat_grad = grad_all.reshape(rows * batches, local_feat)
    halvings = 3 - level_of_batch
    active = (tensor_index < jnp.right_shift(groups, halvings)).astype(jnp.float32)
    active_mask = jnp.tile(active, rows)[:, None]
    chunks = 1
    width = local_cols // chunks
    down_part = None
    normed_part = None
    hiddens, gate_grads, up_grads = [], [], []
    previous = None
    for chunk in range(chunks):
        cols = slice(chunk * width, (chunk + 1) * width)
        gate_w = w_gate[:, cols]
        up_w = w_up[:, cols]
        down_w = w_down[cols, :]
        gate_part = jnp.dot(flat_normed, gate_w, preferred_element_type=jnp.float32)
        up_part = jnp.dot(flat_normed, up_w, preferred_element_type=jnp.float32)
        back_part = lax.dot_general(
            flat_grad, down_w, contract_cols, preferred_element_type=jnp.float32
        )
        parts = (
            gate_part.astype(jnp.bfloat16),
            up_part.astype(jnp.bfloat16),
            back_part.astype(jnp.bfloat16),
        )
        if previous is not None:
            parts, _ = lax.optimization_barrier((parts, previous))
        gate_sum, up_sum, back_sum = lax.psum(parts, "dp")
        previous = (gate_sum, up_sum, back_sum)
        hidden, gate_grad, up_grad = local_terms(
            gate_sum.astype(jnp.float32),
            up_sum.astype(jnp.float32),
            back_sum.astype(jnp.float32),
            active_mask,
        )
        hiddens.append(hidden)
        gate_grads.append(gate_grad)
        up_grads.append(up_grad)
        down_term = jnp.dot(hidden, down_w, preferred_element_type=jnp.float32)
        normed_term = lax.dot_general(
            gate_grad, gate_w, contract_cols, preferred_element_type=jnp.float32
        ) + lax.dot_general(up_grad, up_w, contract_cols, preferred_element_type=jnp.float32)
        down_part = down_term if down_part is None else down_part + down_term
        normed_part = normed_term if normed_part is None else normed_part + normed_term
    hidden = jnp.concatenate(hiddens, axis=1)
    gate_grad = jnp.concatenate(gate_grads, axis=1)
    up_grad = jnp.concatenate(up_grads, axis=1)

    stacked = jnp.stack(
        [
            down_part.reshape(rows, batches, local_feat),
            normed_part.reshape(rows, batches, local_feat),
        ],
        axis=1,
    ).astype(jnp.bfloat16)
    stacked = stacked.reshape(rows, 2 * batches, local_feat)
    shares = lax.psum_scatter(stacked, "tensor", scatter_dimension=0, tiled=True).astype(
        jnp.float32
    )
    shares = shares.reshape(local_rows, 2, batches, local_feat)
    down_output = shares[:, 0].transpose(1, 0, 2)
    normed_grad = shares[:, 1].transpose(1, 0, 2)

    down_out = lax.dot_general(
        hidden, flat_grad, contract_rows, preferred_element_type=jnp.float32
    ).astype(jnp.bfloat16)
    gate_out = lax.dot_general(
        flat_normed, gate_grad, contract_rows, preferred_element_type=jnp.float32
    ).astype(jnp.bfloat16)
    up_out = lax.dot_general(
        flat_normed, up_grad, contract_rows, preferred_element_type=jnp.float32
    ).astype(jnp.bfloat16)

    wide_grad = d_output.astype(jnp.float32)
    weighted = norm_gain * normed_grad
    row_part = jnp.sum(weighted * wide_inputs, axis=2)
    gain_part = jnp.sum(normed_grad * wide_inputs * row_scale[:, :, None], axis=(0, 1))
    row_product = lax.psum(row_part, "dp")
    d_gain = lax.psum(gain_part, "tensor")
    outputs = (wide_inputs + down_output).astype(jnp.bfloat16)
    scale_cube = row_scale * row_scale * row_scale
    d_inputs = (
        wide_grad
        + row_scale[:, :, None] * weighted
        - wide_inputs * (scale_cube * row_product / full_width)[:, :, None]
    ).astype(jnp.bfloat16)
    return (outputs, d_inputs, d_gain, gate_out, up_out, down_out, row_product)


def solution(mesh):
    in_specs = (
        P(None, "tensor", "dp"),
        P("dp"),
        P("dp", "tensor"),
        P("dp", "tensor"),
        P("tensor", "dp"),
        P(None, "tensor", "dp"),
        P(),
    )
    out_specs = (
        P(None, "tensor", "dp"),
        P(None, "tensor", "dp"),
        P("dp"),
        P("dp", "tensor"),
        P("dp", "tensor"),
        P("tensor", "dp"),
        P(None, "tensor"),
    )
    return jax.shard_map(
        per_device, mesh=mesh, in_specs=in_specs, out_specs=out_specs, check_vma=False
    )
```

```python
import jax
import jax.numpy as jnp
from jax import lax
from jax.sharding import PartitionSpec as P

epsilon = 1e-05
contract_cols = (((1,), (1,)), ((), ()))
contract_rows = (((0,), (0,)), ((), ()))


def local_terms(gate_sum, up_sum, back_sum, active_mask):
    sigmoid_gate = jax.nn.sigmoid(gate_sum)
    silu_gate = gate_sum * sigmoid_gate
    slope = sigmoid_gate * (1.0 + gate_sum * (1.0 - sigmoid_gate))
    hidden = (silu_gate * up_sum * active_mask).astype(jnp.bfloat16)
    gate_grad = (back_sum * up_sum * slope * active_mask).astype(jnp.bfloat16)
    up_grad = (back_sum * silu_gate * active_mask).astype(jnp.bfloat16)
    return (hidden, gate_grad, up_grad)


def per_device(inputs, norm_gain, w_gate, w_up, w_down, d_output, level_of_batch):
    groups = lax.axis_size("tensor")
    tensor_index = lax.axis_index("tensor")
    local_feat = w_gate.shape[0]
    local_cols = w_gate.shape[1]
    full_width = local_feat * lax.axis_size("dp")
    batches, local_rows, _ = inputs.shape
    wide_inputs = inputs.astype(jnp.float32)
    square_sum = lax.psum(jnp.sum(wide_inputs * wide_inputs, axis=2), "dp")
    row_scale = lax.rsqrt(square_sum / full_width + epsilon)
    normed = (wide_inputs * row_scale[:, :, None] * norm_gain).astype(jnp.bfloat16)
    both = jnp.concatenate([normed, d_output, inputs], axis=0).transpose(1, 0, 2)
    both_all = lax.all_gather(both, "tensor", axis=0, tiled=True)
    normed_all = both_all[:, :batches]
    grad_all = both_all[:, batches : 2 * batches]
    inputs_all = both_all[:, 2 * batches :].astype(jnp.float32)
    row_scale_all = lax.all_gather(row_scale.T, "tensor", axis=0, tiled=True)
    rows = normed_all.shape[0]

    flat_normed = normed_all.reshape(rows * batches, local_feat)
    flat_grad = grad_all.reshape(rows * batches, local_feat)
    halvings = 3 - level_of_batch
    active = (tensor_index < jnp.right_shift(groups, halvings)).astype(jnp.float32)
    active_mask = jnp.tile(active, rows)[:, None]
    chunks = 1
    width = local_cols // chunks
    down_part = None
    normed_part = None
    hiddens, gate_grads, up_grads = [], [], []
    previous = None
    for chunk in range(chunks):
        cols = slice(chunk * width, (chunk + 1) * width)
        gate_w = w_gate[:, cols]
        up_w = w_up[:, cols]
        down_w = w_down[cols, :]
        gate_part = jnp.dot(flat_normed, gate_w, preferred_element_type=jnp.float32)
        up_part = jnp.dot(flat_normed, up_w, preferred_element_type=jnp.float32)
        back_part = lax.dot_general(
            flat_grad, down_w, contract_cols, preferred_element_type=jnp.float32
        )
        parts = (
            gate_part.astype(jnp.bfloat16),
            up_part.astype(jnp.bfloat16),
            back_part.astype(jnp.bfloat16),
        )
        if previous is not None:
            parts, _ = lax.optimization_barrier((parts, previous))
        gate_sum, up_sum, back_sum = lax.psum(parts, "dp")
        previous = (gate_sum, up_sum, back_sum)
        hidden, gate_grad, up_grad = local_terms(
            gate_sum.astype(jnp.float32),
            up_sum.astype(jnp.float32),
            back_sum.astype(jnp.float32),
            active_mask,
        )
        hiddens.append(hidden)
        gate_grads.append(gate_grad)
        up_grads.append(up_grad)
        down_term = jnp.dot(hidden, down_w, preferred_element_type=jnp.float32)
        normed_term = lax.dot_general(
            gate_grad, gate_w, contract_cols, preferred_element_type=jnp.float32
        ) + lax.dot_general(up_grad, up_w, contract_cols, preferred_element_type=jnp.float32)
        down_part = down_term if down_part is None else down_part + down_term
        normed_part = normed_term if normed_part is None else normed_part + normed_term
    hidden = jnp.concatenate(hiddens, axis=1)
    gate_grad = jnp.concatenate(gate_grads, axis=1)
    up_grad = jnp.concatenate(up_grads, axis=1)

    stacked = jnp.stack(
        [
            down_part.reshape(rows, batches, local_feat),
            normed_part.reshape(rows, batches, local_feat),
        ],
        axis=1,
    ).astype(jnp.bfloat16)
    stacked = stacked.reshape(rows, 2 * batches, local_feat)
    scaled_all = (inputs_all * row_scale_all[:, :, None]).reshape(rows * batches, local_feat)
    d_gain = lax.psum(jnp.sum(normed_part * scaled_all, axis=0), "tensor")
    hidden, flat_grad, _ = lax.optimization_barrier((hidden, flat_grad, stacked))
    shares = lax.psum_scatter(stacked, "tensor", scatter_dimension=0, tiled=True).astype(
        jnp.float32
    )
    shares = shares.reshape(local_rows, 2, batches, local_feat)
    down_output = shares[:, 0].transpose(1, 0, 2)
    normed_grad = shares[:, 1].transpose(1, 0, 2)

    down_out = lax.dot_general(
        hidden, flat_grad, contract_rows, preferred_element_type=jnp.float32
    ).astype(jnp.bfloat16)
    gate_out = lax.dot_general(
        flat_normed, gate_grad, contract_rows, preferred_element_type=jnp.float32
    ).astype(jnp.bfloat16)
    up_out = lax.dot_general(
        flat_normed, up_grad, contract_rows, preferred_element_type=jnp.float32
    ).astype(jnp.bfloat16)

    wide_grad = d_output.astype(jnp.float32)
    weighted = norm_gain * normed_grad
    row_part = jnp.sum(weighted * wide_inputs, axis=2)
    row_product = lax.psum(row_part, "dp")
    outputs = (wide_inputs + down_output).astype(jnp.bfloat16)
    scale_cube = row_scale * row_scale * row_scale
    d_inputs = (
        wide_grad
        + row_scale[:, :, None] * weighted
        - wide_inputs * (scale_cube * row_product / full_width)[:, :, None]
    ).astype(jnp.bfloat16)
    return (outputs, d_inputs, d_gain, gate_out, up_out, down_out, row_product)


def solution(mesh):
    in_specs = (
        P(None, "tensor", "dp"),
        P("dp"),
        P("dp", "tensor"),
        P("dp", "tensor"),
        P("tensor", "dp"),
        P(None, "tensor", "dp"),
        P(),
    )
    out_specs = (
        P(None, "tensor", "dp"),
        P(None, "tensor", "dp"),
        P("dp"),
        P("dp", "tensor"),
        P("dp", "tensor"),
        P("tensor", "dp"),
        P(None, "tensor"),
    )
    return jax.shard_map(
        per_device, mesh=mesh, in_specs=in_specs, out_specs=out_specs, check_vma=False
    )
```

```python
import jax
import jax.numpy as jnp
from jax import lax
from jax.sharding import PartitionSpec as P

epsilon = 1e-05
contract_cols = (((1,), (1,)), ((), ()))
contract_rows = (((0,), (0,)), ((), ()))


def local_terms(gate_sum, up_sum, back_sum, active_mask):
    sigmoid_gate = jax.nn.sigmoid(gate_sum)
    silu_gate = gate_sum * sigmoid_gate
    slope = sigmoid_gate * (1.0 + gate_sum * (1.0 - sigmoid_gate))
    hidden = (silu_gate * up_sum * active_mask).astype(jnp.bfloat16)
    gate_grad = (back_sum * up_sum * slope * active_mask).astype(jnp.bfloat16)
    up_grad = (back_sum * silu_gate * active_mask).astype(jnp.bfloat16)
    return (hidden, gate_grad, up_grad)


def per_device(inputs, norm_gain, w_gate, w_up, w_down, d_output, level_of_batch):
    groups = lax.axis_size("tensor")
    tensor_index = lax.axis_index("tensor")
    local_feat = w_gate.shape[0]
    local_cols = w_gate.shape[1]
    full_width = local_feat * lax.axis_size("dp")
    batches, local_rows, _ = inputs.shape
    wide_inputs = inputs.astype(jnp.float32)
    square_sum = lax.psum(jnp.sum(wide_inputs * wide_inputs, axis=2), "dp")
    row_scale = lax.rsqrt(square_sum / full_width + epsilon)
    normed = (wide_inputs * row_scale[:, :, None] * norm_gain).astype(jnp.bfloat16)
    both = jnp.concatenate([normed, d_output, inputs], axis=0).transpose(1, 0, 2)
    both_all = lax.all_gather(both, "tensor", axis=0, tiled=True)
    normed_all = both_all[:, :batches]
    grad_all = both_all[:, batches : 2 * batches]
    inputs_all = both_all[:, 2 * batches :].astype(jnp.float32)
    row_scale_all = lax.all_gather(row_scale.T, "tensor", axis=0, tiled=True)
    rows = normed_all.shape[0]
    start = tensor_index * local_rows

    flat_normed = normed_all.reshape(rows * batches, local_feat)
    flat_grad = grad_all.reshape(rows * batches, local_feat)
    halvings = 3 - level_of_batch
    active = (tensor_index < jnp.right_shift(groups, halvings)).astype(jnp.float32)
    active_mask = jnp.tile(active, rows)[:, None]
    chunks = 1
    width = local_cols // chunks
    down_part = None
    normed_part = None
    hiddens, gate_grads, up_grads = [], [], []
    previous = None
    for chunk in range(chunks):
        cols = slice(chunk * width, (chunk + 1) * width)
        gate_w = w_gate[:, cols]
        up_w = w_up[:, cols]
        down_w = w_down[cols, :]
        gate_part = jnp.dot(flat_normed, gate_w, preferred_element_type=jnp.float32)
        up_part = jnp.dot(flat_normed, up_w, preferred_element_type=jnp.float32)
        back_part = lax.dot_general(
            flat_grad, down_w, contract_cols, preferred_element_type=jnp.float32
        )
        parts = (
            gate_part.astype(jnp.bfloat16),
            up_part.astype(jnp.bfloat16),
            back_part.astype(jnp.bfloat16),
        )
        if previous is not None:
            parts, _ = lax.optimization_barrier((parts, previous))
        gate_sum, up_sum, back_sum = lax.psum(parts, "dp")
        previous = (gate_sum, up_sum, back_sum)
        hidden, gate_grad, up_grad = local_terms(
            gate_sum.astype(jnp.float32),
            up_sum.astype(jnp.float32),
            back_sum.astype(jnp.float32),
            active_mask,
        )
        hiddens.append(hidden)
        gate_grads.append(gate_grad)
        up_grads.append(up_grad)
        down_term = jnp.dot(hidden, down_w, preferred_element_type=jnp.float32)
        normed_term = lax.dot_general(
            gate_grad, gate_w, contract_cols, preferred_element_type=jnp.float32
        ) + lax.dot_general(up_grad, up_w, contract_cols, preferred_element_type=jnp.float32)
        down_part = down_term if down_part is None else down_part + down_term
        normed_part = normed_term if normed_part is None else normed_part + normed_term
    hidden = jnp.concatenate(hiddens, axis=1)
    gate_grad = jnp.concatenate(gate_grads, axis=1)
    up_grad = jnp.concatenate(up_grads, axis=1)

    stacked = jnp.stack(
        [
            down_part.reshape(rows, batches, local_feat),
            normed_part.reshape(rows, batches, local_feat),
        ],
        axis=1,
    ).astype(jnp.bfloat16)
    stacked = stacked.reshape(rows, 2 * batches, local_feat)
    scaled_all = (inputs_all * row_scale_all[:, :, None]).reshape(rows * batches, local_feat)
    gain_part = jnp.sum(normed_part * scaled_all, axis=0)
    row_all = jnp.sum(
        normed_part * (norm_gain * inputs_all.reshape(rows * batches, local_feat)), axis=1
    )
    reduced = lax.psum(jnp.concatenate([gain_part, row_all]), "tensor")
    d_gain = reduced[:local_feat]
    row_all = lax.psum(reduced[local_feat:], "dp").reshape(rows, batches)
    row_product = lax.dynamic_slice_in_dim(row_all, start, local_rows, axis=0).T
    hidden, flat_grad, _ = lax.optimization_barrier((hidden, flat_grad, stacked))
    shares = lax.psum_scatter(stacked, "tensor", scatter_dimension=0, tiled=True).astype(
        jnp.float32
    )
    shares = shares.reshape(local_rows, 2, batches, local_feat)
    down_output = shares[:, 0].transpose(1, 0, 2)
    normed_grad = shares[:, 1].transpose(1, 0, 2)

    down_out = lax.dot_general(
        hidden, flat_grad, contract_rows, preferred_element_type=jnp.float32
    ).astype(jnp.bfloat16)
    gate_out = lax.dot_general(
        flat_normed, gate_grad, contract_rows, preferred_element_type=jnp.float32
    ).astype(jnp.bfloat16)
    up_out = lax.dot_general(
        flat_normed, up_grad, contract_rows, preferred_element_type=jnp.float32
    ).astype(jnp.bfloat16)

    wide_grad = d_output.astype(jnp.float32)
    weighted = norm_gain * normed_grad
    outputs = (wide_inputs + down_output).astype(jnp.bfloat16)
    scale_cube = row_scale * row_scale * row_scale
    d_inputs = (
        wide_grad
        + row_scale[:, :, None] * weighted
        - wide_inputs * (scale_cube * row_product / full_width)[:, :, None]
    ).astype(jnp.bfloat16)
    return (outputs, d_inputs, d_gain, gate_out, up_out, down_out, row_product)


def solution(mesh):
    in_specs = (
        P(None, "tensor", "dp"),
        P("dp"),
        P("dp", "tensor"),
        P("dp", "tensor"),
        P("tensor", "dp"),
        P(None, "tensor", "dp"),
        P(),
    )
    out_specs = (
        P(None, "tensor", "dp"),
        P(None, "tensor", "dp"),
        P("dp"),
        P("dp", "tensor"),
        P("dp", "tensor"),
        P("tensor", "dp"),
        P(None, "tensor"),
    )
    return jax.shard_map(
        per_device, mesh=mesh, in_specs=in_specs, out_specs=out_specs, check_vma=False
    )
```

```python
import jax
import jax.numpy as jnp
from jax import lax
from jax.sharding import PartitionSpec as P

epsilon = 1e-05
contract_cols = (((1,), (1,)), ((), ()))
contract_rows = (((0,), (0,)), ((), ()))


def local_terms(gate_sum, up_sum, back_sum, active_mask):
    sigmoid_gate = jax.nn.sigmoid(gate_sum)
    silu_gate = gate_sum * sigmoid_gate
    slope = sigmoid_gate * (1.0 + gate_sum * (1.0 - sigmoid_gate))
    hidden = (silu_gate * up_sum * active_mask).astype(jnp.bfloat16)
    gate_grad = (back_sum * up_sum * slope * active_mask).astype(jnp.bfloat16)
    up_grad = (back_sum * silu_gate * active_mask).astype(jnp.bfloat16)
    return (hidden, gate_grad, up_grad)


def per_device(inputs, norm_gain, w_gate, w_up, w_down, d_output, level_of_batch):
    groups = lax.axis_size("tensor")
    tensor_index = lax.axis_index("tensor")
    local_feat = w_gate.shape[0]
    local_cols = w_gate.shape[1]
    full_width = local_feat * lax.axis_size("dp")
    batches, local_rows, _ = inputs.shape
    wide_inputs = inputs.astype(jnp.float32)
    square_sum = lax.psum(jnp.sum(wide_inputs * wide_inputs, axis=2), "dp")
    row_scale = lax.rsqrt(square_sum / full_width + epsilon)
    normed = (wide_inputs * row_scale[:, :, None] * norm_gain).astype(jnp.bfloat16)
    both = jnp.concatenate([normed, d_output, inputs], axis=0).transpose(1, 0, 2)
    both_all = lax.all_gather(both, "tensor", axis=0, tiled=True)
    normed_all = both_all[:, :batches]
    grad_all = both_all[:, batches : 2 * batches]
    inputs_all = both_all[:, 2 * batches :].astype(jnp.float32)
    row_scale_all = lax.all_gather(row_scale.T, "tensor", axis=0, tiled=True)
    rows = normed_all.shape[0]
    start = tensor_index * local_rows

    flat_normed = normed_all.reshape(rows * batches, local_feat)
    flat_grad = grad_all.reshape(rows * batches, local_feat)
    halvings = 3 - level_of_batch
    active = (tensor_index < jnp.right_shift(groups, halvings)).astype(jnp.float32)
    active_mask = jnp.tile(active, rows)[:, None]
    chunks = 1
    width = local_cols // chunks
    down_part = None
    normed_part = None
    hiddens, gate_grads, up_grads = [], [], []
    previous = None
    for chunk in range(chunks):
        cols = slice(chunk * width, (chunk + 1) * width)
        gate_w = w_gate[:, cols]
        up_w = w_up[:, cols]
        down_w = w_down[cols, :]
        gate_part = jnp.dot(flat_normed, gate_w, preferred_element_type=jnp.float32)
        up_part = jnp.dot(flat_normed, up_w, preferred_element_type=jnp.float32)
        back_part = lax.dot_general(
            flat_grad, down_w, contract_cols, preferred_element_type=jnp.float32
        )
        parts = (
            gate_part.astype(jnp.bfloat16),
            up_part.astype(jnp.bfloat16),
            back_part.astype(jnp.bfloat16),
        )
        if previous is not None:
            parts, _ = lax.optimization_barrier((parts, previous))
        gate_sum, up_sum, back_sum = lax.psum(parts, "dp")
        previous = (gate_sum, up_sum, back_sum)
        hidden, gate_grad, up_grad = local_terms(
            gate_sum.astype(jnp.float32),
            up_sum.astype(jnp.float32),
            back_sum.astype(jnp.float32),
            active_mask,
        )
        hidden, gate_grad, up_grad = lax.optimization_barrier((hidden, gate_grad, up_grad))
        hiddens.append(hidden)
        gate_grads.append(gate_grad)
        up_grads.append(up_grad)
        down_term = jnp.dot(hidden, down_w, preferred_element_type=jnp.float32)
        normed_term = lax.dot_general(
            gate_grad, gate_w, contract_cols, preferred_element_type=jnp.float32
        ) + lax.dot_general(up_grad, up_w, contract_cols, preferred_element_type=jnp.float32)
        down_part = down_term if down_part is None else down_part + down_term
        normed_part = normed_term if normed_part is None else normed_part + normed_term
    hidden = jnp.concatenate(hiddens, axis=1)
    gate_grad = jnp.concatenate(gate_grads, axis=1)
    up_grad = jnp.concatenate(up_grads, axis=1)

    stacked = jnp.stack(
        [
            down_part.reshape(rows, batches, local_feat),
            normed_part.reshape(rows, batches, local_feat),
        ],
        axis=1,
    ).astype(jnp.bfloat16)
    stacked = stacked.reshape(rows, 2 * batches, local_feat)
    scaled_all = (inputs_all * row_scale_all[:, :, None]).reshape(rows * batches, local_feat)
    gain_part = jnp.sum(normed_part * scaled_all, axis=0)
    row_all = jnp.sum(
        normed_part * (norm_gain * inputs_all.reshape(rows * batches, local_feat)), axis=1
    )
    reduced = lax.psum(jnp.concatenate([gain_part, row_all]), "tensor")
    d_gain = reduced[:local_feat]
    row_all = lax.psum(reduced[local_feat:], "dp").reshape(rows, batches)
    row_product = lax.dynamic_slice_in_dim(row_all, start, local_rows, axis=0).T
    hidden, flat_grad, _ = lax.optimization_barrier((hidden, flat_grad, stacked))
    shares = lax.psum_scatter(stacked, "tensor", scatter_dimension=0, tiled=True).astype(
        jnp.float32
    )
    shares = shares.reshape(local_rows, 2, batches, local_feat)
    down_output = shares[:, 0].transpose(1, 0, 2)
    normed_grad = shares[:, 1].transpose(1, 0, 2)

    down_out = lax.dot_general(
        hidden, flat_grad, contract_rows, preferred_element_type=jnp.float32
    ).astype(jnp.bfloat16)
    gate_out = lax.dot_general(
        flat_normed, gate_grad, contract_rows, preferred_element_type=jnp.float32
    ).astype(jnp.bfloat16)
    up_out = lax.dot_general(
        flat_normed, up_grad, contract_rows, preferred_element_type=jnp.float32
    ).astype(jnp.bfloat16)

    wide_grad = d_output.astype(jnp.float32)
    weighted = norm_gain * normed_grad
    outputs = (wide_inputs + down_output).astype(jnp.bfloat16)
    scale_cube = row_scale * row_scale * row_scale
    d_inputs = (
        wide_grad
        + row_scale[:, :, None] * weighted
        - wide_inputs * (scale_cube * row_product / full_width)[:, :, None]
    ).astype(jnp.bfloat16)
    return (outputs, d_inputs, d_gain, gate_out, up_out, down_out, row_product)


def solution(mesh):
    in_specs = (
        P(None, "tensor", "dp"),
        P("dp"),
        P("dp", "tensor"),
        P("dp", "tensor"),
        P("tensor", "dp"),
        P(None, "tensor", "dp"),
        P(),
    )
    out_specs = (
        P(None, "tensor", "dp"),
        P(None, "tensor", "dp"),
        P("dp"),
        P("dp", "tensor"),
        P("dp", "tensor"),
        P("tensor", "dp"),
        P(None, "tensor"),
    )
    return jax.shard_map(
        per_device, mesh=mesh, in_specs=in_specs, out_specs=out_specs, check_vma=False
    )
```

```python
import jax
import jax.numpy as jnp
from jax import lax
from jax.sharding import PartitionSpec as P

epsilon = 1e-05
contract_cols = (((1,), (1,)), ((), ()))
contract_rows = (((0,), (0,)), ((), ()))


def local_terms(gate_sum, up_sum, back_sum, active_mask):
    sigmoid_gate = jax.nn.sigmoid(gate_sum)
    silu_gate = gate_sum * sigmoid_gate
    slope = sigmoid_gate * (1.0 + gate_sum * (1.0 - sigmoid_gate))
    hidden = (silu_gate * up_sum * active_mask).astype(jnp.bfloat16)
    gate_grad = (back_sum * up_sum * slope * active_mask).astype(jnp.bfloat16)
    up_grad = (back_sum * silu_gate * active_mask).astype(jnp.bfloat16)
    return (hidden, gate_grad, up_grad)


def per_device(inputs, norm_gain, w_gate, w_up, w_down, d_output, level_of_batch):
    groups = lax.axis_size("tensor")
    tensor_index = lax.axis_index("tensor")
    local_feat = w_gate.shape[0]
    local_cols = w_gate.shape[1]
    full_width = local_feat * lax.axis_size("dp")
    batches, local_rows, _ = inputs.shape
    wide_inputs = inputs.astype(jnp.float32)
    both = jnp.concatenate([d_output, inputs], axis=0).transpose(1, 0, 2)
    both_all = lax.all_gather(both, "tensor", axis=0, tiled=True)
    grad_all = both_all[:, :batches]
    inputs_all = both_all[:, batches:].astype(jnp.float32)
    rows = grad_all.shape[0]
    start = tensor_index * local_rows
    flat_grad = grad_all.reshape(rows * batches, local_feat)
    back_first = lax.psum(
        lax.dot_general(
            flat_grad, w_down, contract_cols, preferred_element_type=jnp.float32
        ).astype(jnp.bfloat16),
        "dp",
    )
    square_sum = lax.psum(jnp.sum(inputs_all * inputs_all, axis=2).T, "dp").T
    row_scale_all = lax.rsqrt(square_sum / full_width + epsilon)
    normed_all = (inputs_all * row_scale_all[:, :, None] * norm_gain).astype(jnp.bfloat16)
    row_scale = lax.dynamic_slice_in_dim(row_scale_all, start, local_rows, axis=0).T

    flat_normed = normed_all.reshape(rows * batches, local_feat)
    halvings = 3 - level_of_batch
    active = (tensor_index < jnp.right_shift(groups, halvings)).astype(jnp.float32)
    active_mask = jnp.tile(active, rows)[:, None]
    chunks = 1
    width = local_cols // chunks
    down_part = None
    normed_part = None
    hiddens, gate_grads, up_grads = [], [], []
    for chunk in range(chunks):
        cols = slice(chunk * width, (chunk + 1) * width)
        gate_w = w_gate[:, cols]
        up_w = w_up[:, cols]
        down_w = w_down[cols, :]
        gate_part = jnp.dot(flat_normed, gate_w, preferred_element_type=jnp.float32)
        up_part = jnp.dot(flat_normed, up_w, preferred_element_type=jnp.float32)
        parts = (gate_part.astype(jnp.bfloat16), up_part.astype(jnp.bfloat16))
        parts, back_sum = lax.optimization_barrier((parts, back_first))
        gate_sum, up_sum = lax.psum(parts, "dp")
        hidden, gate_grad, up_grad = local_terms(
            gate_sum.astype(jnp.float32),
            up_sum.astype(jnp.float32),
            back_sum.astype(jnp.float32),
            active_mask,
        )
        hiddens.append(hidden)
        gate_grads.append(gate_grad)
        up_grads.append(up_grad)
        down_term = jnp.dot(hidden, down_w, preferred_element_type=jnp.float32)
        normed_term = lax.dot_general(
            gate_grad, gate_w, contract_cols, preferred_element_type=jnp.float32
        ) + lax.dot_general(up_grad, up_w, contract_cols, preferred_element_type=jnp.float32)
        down_part = down_term if down_part is None else down_part + down_term
        normed_part = normed_term if normed_part is None else normed_part + normed_term
    hidden = jnp.concatenate(hiddens, axis=1)
    gate_grad = jnp.concatenate(gate_grads, axis=1)
    up_grad = jnp.concatenate(up_grads, axis=1)

    stacked = jnp.stack(
        [
            down_part.reshape(rows, batches, local_feat),
            normed_part.reshape(rows, batches, local_feat),
        ],
        axis=1,
    ).astype(jnp.bfloat16)
    stacked = stacked.reshape(rows, 2 * batches, local_feat)
    scaled_all = (inputs_all * row_scale_all[:, :, None]).reshape(rows * batches, local_feat)
    gain_part = jnp.sum(normed_part * scaled_all, axis=0)
    row_all = jnp.sum(
        normed_part * (norm_gain * inputs_all.reshape(rows * batches, local_feat)), axis=1
    )
    reduced = lax.psum(jnp.concatenate([gain_part, row_all]), "tensor")
    d_gain = reduced[:local_feat]
    row_all = lax.psum(reduced[local_feat:], "dp").reshape(rows, batches)
    row_product = lax.dynamic_slice_in_dim(row_all, start, local_rows, axis=0).T
    hidden, flat_grad, _ = lax.optimization_barrier((hidden, flat_grad, stacked))
    shares = lax.psum_scatter(stacked, "tensor", scatter_dimension=0, tiled=True).astype(
        jnp.float32
    )
    shares = shares.reshape(local_rows, 2, batches, local_feat)
    down_output = shares[:, 0].transpose(1, 0, 2)
    normed_grad = shares[:, 1].transpose(1, 0, 2)

    down_out = lax.dot_general(
        hidden, flat_grad, contract_rows, preferred_element_type=jnp.float32
    ).astype(jnp.bfloat16)
    gate_out = lax.dot_general(
        flat_normed, gate_grad, contract_rows, preferred_element_type=jnp.float32
    ).astype(jnp.bfloat16)
    up_out = lax.dot_general(
        flat_normed, up_grad, contract_rows, preferred_element_type=jnp.float32
    ).astype(jnp.bfloat16)

    wide_grad = d_output.astype(jnp.float32)
    weighted = norm_gain * normed_grad
    outputs = (wide_inputs + down_output).astype(jnp.bfloat16)
    scale_cube = row_scale * row_scale * row_scale
    d_inputs = (
        wide_grad
        + row_scale[:, :, None] * weighted
        - wide_inputs * (scale_cube * row_product / full_width)[:, :, None]
    ).astype(jnp.bfloat16)
    return (outputs, d_inputs, d_gain, gate_out, up_out, down_out, row_product)


def solution(mesh):
    in_specs = (
        P(None, "tensor", "dp"),
        P("dp"),
        P("dp", "tensor"),
        P("dp", "tensor"),
        P("tensor", "dp"),
        P(None, "tensor", "dp"),
        P(),
    )
    out_specs = (
        P(None, "tensor", "dp"),
        P(None, "tensor", "dp"),
        P("dp"),
        P("dp", "tensor"),
        P("dp", "tensor"),
        P("tensor", "dp"),
        P(None, "tensor"),
    )
    return jax.shard_map(
        per_device, mesh=mesh, in_specs=in_specs, out_specs=out_specs, check_vma=False
    )
```

```python
import jax
import jax.numpy as jnp
from jax import lax
from jax.experimental import pallas as pl
from jax.sharding import PartitionSpec as P

epsilon = 1e-05
contract_cols = (((1,), (1,)), ((), ()))
contract_rows = (((0,), (0,)), ((), ()))


def local_terms(gate_sum, up_sum, back_sum, active_mask):
    sigmoid_gate = jax.nn.sigmoid(gate_sum)
    silu_gate = gate_sum * sigmoid_gate
    slope = sigmoid_gate * (1.0 + gate_sum * (1.0 - sigmoid_gate))
    hidden = (silu_gate * up_sum * active_mask).astype(jnp.bfloat16)
    gate_grad = (back_sum * up_sum * slope * active_mask).astype(jnp.bfloat16)
    up_grad = (back_sum * silu_gate * active_mask).astype(jnp.bfloat16)
    return (hidden, gate_grad, up_grad)


def outer_kernel(left_ref, right_ref, out_ref):
    out_ref[...] = lax.dot_general(
        left_ref[...], right_ref[...], contract_rows, preferred_element_type=jnp.float32
    ).astype(out_ref.dtype)


def outer_product(left, right):
    depth, m = left.shape
    n = right.shape[1]
    if n >= m:
        tile = n // 2 if n % 256 == 0 else n
        grid = (n // tile,)
        in_specs = [
            pl.BlockSpec((depth, m), lambda j: (0, 0)),
            pl.BlockSpec((depth, tile), lambda j: (0, j)),
        ]
        out_specs = pl.BlockSpec((m, tile), lambda j: (0, j))
    else:
        tile = m // 2 if m % 256 == 0 else m
        grid = (m // tile,)
        in_specs = [
            pl.BlockSpec((depth, tile), lambda i: (0, i)),
            pl.BlockSpec((depth, n), lambda i: (0, 0)),
        ]
        out_specs = pl.BlockSpec((tile, n), lambda i: (i, 0))
    return pl.pallas_call(
        outer_kernel,
        grid=grid,
        in_specs=in_specs,
        out_specs=out_specs,
        out_shape=jax.ShapeDtypeStruct((m, n), jnp.bfloat16),
        cost_estimate=pl.CostEstimate(
            flops=2 * depth * m * n,
            bytes_accessed=2 * (depth * m + depth * n + m * n),
            transcendentals=0,
        ),
    )(left, right)


def per_device(inputs, norm_gain, w_gate, w_up, w_down, d_output, level_of_batch):
    groups = lax.axis_size("tensor")
    tensor_index = lax.axis_index("tensor")
    local_feat = w_gate.shape[0]
    local_cols = w_gate.shape[1]
    full_width = local_feat * lax.axis_size("dp")
    batches, local_rows, _ = inputs.shape
    wide_inputs = inputs.astype(jnp.float32)
    both = jnp.concatenate([d_output, inputs], axis=0).transpose(1, 0, 2)
    both_all = lax.all_gather(both, "tensor", axis=0, tiled=True)
    grad_all = both_all[:, :batches]
    inputs_all = both_all[:, batches:].astype(jnp.float32)
    rows = grad_all.shape[0]
    start = tensor_index * local_rows
    flat_grad = grad_all.reshape(rows * batches, local_feat)
    back_first = lax.psum(
        lax.dot_general(
            flat_grad, w_down, contract_cols, preferred_element_type=jnp.float32
        ).astype(jnp.bfloat16),
        "dp",
    )
    square_sum = lax.psum(jnp.sum(inputs_all * inputs_all, axis=2).T, "dp").T
    row_scale_all = lax.rsqrt(square_sum / full_width + epsilon)
    normed_all = (inputs_all * row_scale_all[:, :, None] * norm_gain).astype(jnp.bfloat16)
    row_scale = lax.dynamic_slice_in_dim(row_scale_all, start, local_rows, axis=0).T

    flat_normed = normed_all.reshape(rows * batches, local_feat)
    halvings = 3 - level_of_batch
    active = (tensor_index < jnp.right_shift(groups, halvings)).astype(jnp.float32)
    active_mask = jnp.tile(active, rows)[:, None]
    chunks = 1
    width = local_cols // chunks
    down_part = None
    normed_part = None
    hiddens, gate_grads, up_grads = [], [], []
    for chunk in range(chunks):
        cols = slice(chunk * width, (chunk + 1) * width)
        gate_w = w_gate[:, cols]
        up_w = w_up[:, cols]
        down_w = w_down[cols, :]
        gate_part = jnp.dot(flat_normed, gate_w, preferred_element_type=jnp.float32)
        up_part = jnp.dot(flat_normed, up_w, preferred_element_type=jnp.float32)
        parts = (gate_part.astype(jnp.bfloat16), up_part.astype(jnp.bfloat16))
        parts, back_sum = lax.optimization_barrier((parts, back_first))
        gate_sum, up_sum = lax.psum(parts, "dp")
        hidden, gate_grad, up_grad = local_terms(
            gate_sum.astype(jnp.float32),
            up_sum.astype(jnp.float32),
            back_sum.astype(jnp.float32),
            active_mask,
        )
        hiddens.append(hidden)
        gate_grads.append(gate_grad)
        up_grads.append(up_grad)
        down_term = jnp.dot(hidden, down_w, preferred_element_type=jnp.float32)
        normed_term = lax.dot_general(
            gate_grad, gate_w, contract_cols, preferred_element_type=jnp.float32
        ) + lax.dot_general(up_grad, up_w, contract_cols, preferred_element_type=jnp.float32)
        down_part = down_term if down_part is None else down_part + down_term
        normed_part = normed_term if normed_part is None else normed_part + normed_term
    hidden = jnp.concatenate(hiddens, axis=1)
    gate_grad = jnp.concatenate(gate_grads, axis=1)
    up_grad = jnp.concatenate(up_grads, axis=1)

    stacked = jnp.stack(
        [
            down_part.reshape(rows, batches, local_feat),
            normed_part.reshape(rows, batches, local_feat),
        ],
        axis=1,
    ).astype(jnp.bfloat16)
    stacked = stacked.reshape(rows, 2 * batches, local_feat)
    scaled_all = (inputs_all * row_scale_all[:, :, None]).reshape(rows * batches, local_feat)
    gain_part = jnp.sum(normed_part * scaled_all, axis=0)
    row_all = jnp.sum(
        normed_part * (norm_gain * inputs_all.reshape(rows * batches, local_feat)), axis=1
    )
    reduced = lax.psum(jnp.concatenate([gain_part, row_all]), "tensor")
    d_gain = reduced[:local_feat]
    row_all = lax.psum(reduced[local_feat:], "dp").reshape(rows, batches)
    row_product = lax.dynamic_slice_in_dim(row_all, start, local_rows, axis=0).T
    hidden, flat_grad, _ = lax.optimization_barrier((hidden, flat_grad, stacked))
    shares = lax.psum_scatter(stacked, "tensor", scatter_dimension=0, tiled=True).astype(
        jnp.float32
    )
    shares = shares.reshape(local_rows, 2, batches, local_feat)
    down_output = shares[:, 0].transpose(1, 0, 2)
    normed_grad = shares[:, 1].transpose(1, 0, 2)

    down_out = outer_product(hidden, flat_grad)
    gate_out = outer_product(flat_normed, gate_grad)
    up_out = outer_product(flat_normed, up_grad)

    wide_grad = d_output.astype(jnp.float32)
    weighted = norm_gain * normed_grad
    outputs = (wide_inputs + down_output).astype(jnp.bfloat16)
    scale_cube = row_scale * row_scale * row_scale
    d_inputs = (
        wide_grad
        + row_scale[:, :, None] * weighted
        - wide_inputs * (scale_cube * row_product / full_width)[:, :, None]
    ).astype(jnp.bfloat16)
    return (outputs, d_inputs, d_gain, gate_out, up_out, down_out, row_product)


def solution(mesh):
    in_specs = (
        P(None, "tensor", "dp"),
        P("dp"),
        P("dp", "tensor"),
        P("dp", "tensor"),
        P("tensor", "dp"),
        P(None, "tensor", "dp"),
        P(),
    )
    out_specs = (
        P(None, "tensor", "dp"),
        P(None, "tensor", "dp"),
        P("dp"),
        P("dp", "tensor"),
        P("dp", "tensor"),
        P("tensor", "dp"),
        P(None, "tensor"),
    )
    return jax.shard_map(
        per_device, mesh=mesh, in_specs=in_specs, out_specs=out_specs, check_vma=False
    )
```

```python
import jax
import jax.numpy as jnp
from jax import lax
from jax.sharding import PartitionSpec as P

epsilon = 1e-05
contract_cols = (((1,), (1,)), ((), ()))
contract_rows = (((0,), (0,)), ((), ()))


def local_terms(gate_sum, up_sum, back_sum, active_mask):
    sigmoid_gate = jax.nn.sigmoid(gate_sum)
    silu_gate = gate_sum * sigmoid_gate
    slope = sigmoid_gate * (1.0 + gate_sum * (1.0 - sigmoid_gate))
    hidden = (silu_gate * up_sum * active_mask).astype(jnp.bfloat16)
    gate_grad = (back_sum * up_sum * slope * active_mask).astype(jnp.bfloat16)
    up_grad = (back_sum * silu_gate * active_mask).astype(jnp.bfloat16)
    return (hidden, gate_grad, up_grad)


def per_device(inputs, norm_gain, w_gate, w_up, w_down, d_output, level_of_batch):
    groups = lax.axis_size("tensor")
    tensor_index = lax.axis_index("tensor")
    local_feat = w_gate.shape[0]
    local_cols = w_gate.shape[1]
    full_width = local_feat * lax.axis_size("dp")
    batches, local_rows, _ = inputs.shape
    wide_inputs = inputs.astype(jnp.float32)
    grad_all = lax.all_gather(d_output.transpose(1, 0, 2), "tensor", axis=0, tiled=True)
    rows = grad_all.shape[0]
    start = tensor_index * local_rows
    flat_grad = grad_all.reshape(rows * batches, local_feat)
    back_part = lax.dot_general(
        flat_grad, w_down, contract_cols, preferred_element_type=jnp.float32
    ).astype(jnp.bfloat16)
    back_first = lax.psum(back_part, "dp")
    inputs_all, _ = lax.optimization_barrier((inputs.transpose(1, 0, 2), back_part))
    inputs_all = lax.all_gather(inputs_all, "tensor", axis=0, tiled=True).astype(jnp.float32)
    square_sum = lax.psum(jnp.sum(inputs_all * inputs_all, axis=2).T, "dp").T
    row_scale_all = lax.rsqrt(square_sum / full_width + epsilon)
    normed_all = (inputs_all * row_scale_all[:, :, None] * norm_gain).astype(jnp.bfloat16)
    row_scale = lax.dynamic_slice_in_dim(row_scale_all, start, local_rows, axis=0).T

    flat_normed = normed_all.reshape(rows * batches, local_feat)
    halvings = 3 - level_of_batch
    active = (tensor_index < jnp.right_shift(groups, halvings)).astype(jnp.float32)
    active_mask = jnp.tile(active, rows)[:, None]
    chunks = 1
    width = local_cols // chunks
    down_part = None
    normed_part = None
    hiddens, gate_grads, up_grads = [], [], []
    for chunk in range(chunks):
        cols = slice(chunk * width, (chunk + 1) * width)
        gate_w = w_gate[:, cols]
        up_w = w_up[:, cols]
        down_w = w_down[cols, :]
        gate_part = jnp.dot(flat_normed, gate_w, preferred_element_type=jnp.float32)
        up_part = jnp.dot(flat_normed, up_w, preferred_element_type=jnp.float32)
        parts = (gate_part.astype(jnp.bfloat16), up_part.astype(jnp.bfloat16))
        parts, back_sum = lax.optimization_barrier((parts, back_first))
        gate_sum, up_sum = lax.psum(parts, "dp")
        hidden, gate_grad, up_grad = local_terms(
            gate_sum.astype(jnp.float32),
            up_sum.astype(jnp.float32),
            back_sum.astype(jnp.float32),
            active_mask,
        )
        hiddens.append(hidden)
        gate_grads.append(gate_grad)
        up_grads.append(up_grad)
        down_term = jnp.dot(hidden, down_w, preferred_element_type=jnp.float32)
        normed_term = lax.dot_general(
            gate_grad, gate_w, contract_cols, preferred_element_type=jnp.float32
        ) + lax.dot_general(up_grad, up_w, contract_cols, preferred_element_type=jnp.float32)
        down_part = down_term if down_part is None else down_part + down_term
        normed_part = normed_term if normed_part is None else normed_part + normed_term
    hidden = jnp.concatenate(hiddens, axis=1)
    gate_grad = jnp.concatenate(gate_grads, axis=1)
    up_grad = jnp.concatenate(up_grads, axis=1)

    stacked = jnp.stack(
        [
            down_part.reshape(rows, batches, local_feat),
            normed_part.reshape(rows, batches, local_feat),
        ],
        axis=1,
    ).astype(jnp.bfloat16)
    stacked = stacked.reshape(rows, 2 * batches, local_feat)
    scaled_all = (inputs_all * row_scale_all[:, :, None]).reshape(rows * batches, local_feat)
    gain_part = jnp.sum(normed_part * scaled_all, axis=0)
    row_all = jnp.sum(
        normed_part * (norm_gain * inputs_all.reshape(rows * batches, local_feat)), axis=1
    )
    reduced = lax.psum(jnp.concatenate([gain_part, row_all]), "tensor")
    d_gain = reduced[:local_feat]
    row_all = lax.psum(reduced[local_feat:], "dp").reshape(rows, batches)
    row_product = lax.dynamic_slice_in_dim(row_all, start, local_rows, axis=0).T
    hidden, flat_grad, _ = lax.optimization_barrier((hidden, flat_grad, stacked))
    shares = lax.psum_scatter(stacked, "tensor", scatter_dimension=0, tiled=True).astype(
        jnp.float32
    )
    shares = shares.reshape(local_rows, 2, batches, local_feat)
    down_output = shares[:, 0].transpose(1, 0, 2)
    normed_grad = shares[:, 1].transpose(1, 0, 2)

    down_out = lax.dot_general(
        hidden, flat_grad, contract_rows, preferred_element_type=jnp.float32
    ).astype(jnp.bfloat16)
    gate_out = lax.dot_general(
        flat_normed, gate_grad, contract_rows, preferred_element_type=jnp.float32
    ).astype(jnp.bfloat16)
    up_out = lax.dot_general(
        flat_normed, up_grad, contract_rows, preferred_element_type=jnp.float32
    ).astype(jnp.bfloat16)

    wide_grad = d_output.astype(jnp.float32)
    weighted = norm_gain * normed_grad
    outputs = (wide_inputs + down_output).astype(jnp.bfloat16)
    scale_cube = row_scale * row_scale * row_scale
    d_inputs = (
        wide_grad
        + row_scale[:, :, None] * weighted
        - wide_inputs * (scale_cube * row_product / full_width)[:, :, None]
    ).astype(jnp.bfloat16)
    return (outputs, d_inputs, d_gain, gate_out, up_out, down_out, row_product)


def solution(mesh):
    in_specs = (
        P(None, "tensor", "dp"),
        P("dp"),
        P("dp", "tensor"),
        P("dp", "tensor"),
        P("tensor", "dp"),
        P(None, "tensor", "dp"),
        P(),
    )
    out_specs = (
        P(None, "tensor", "dp"),
        P(None, "tensor", "dp"),
        P("dp"),
        P("dp", "tensor"),
        P("dp", "tensor"),
        P("tensor", "dp"),
        P(None, "tensor"),
    )
    return jax.shard_map(
        per_device, mesh=mesh, in_specs=in_specs, out_specs=out_specs, check_vma=False
    )
```

```python
import functools

import jax
import jax.numpy as jnp
from jax import lax
from jax.sharding import PartitionSpec as P

epsilon = 1e-05
contract_cols = (((1,), (1,)), ((), ()))
contract_rows = (((0,), (0,)), ((), ()))


def local_terms(gate_sum, up_sum, back_sum, active_mask):
    sigmoid_gate = jax.nn.sigmoid(gate_sum)
    silu_gate = gate_sum * sigmoid_gate
    slope = sigmoid_gate * (1.0 + gate_sum * (1.0 - sigmoid_gate))
    hidden = (silu_gate * up_sum * active_mask).astype(jnp.bfloat16)
    gate_grad = (back_sum * up_sum * slope * active_mask).astype(jnp.bfloat16)
    up_grad = (back_sum * silu_gate * active_mask).astype(jnp.bfloat16)
    return (hidden, gate_grad, up_grad)


def per_device(inputs, norm_gain, w_gate, w_up, w_down, d_output, level_of_batch):
    groups = lax.axis_size("tensor")
    tensor_index = lax.axis_index("tensor")
    local_feat = w_gate.shape[0]
    local_cols = w_gate.shape[1]
    full_width = local_feat * lax.axis_size("dp")
    batches, local_rows, _ = inputs.shape
    wide_inputs = inputs.astype(jnp.float32)
    grad_all = lax.all_gather(d_output.transpose(1, 0, 2), "tensor", axis=0, tiled=True)
    rows = grad_all.shape[0]
    start = tensor_index * local_rows
    flat_grad = grad_all.reshape(rows * batches, local_feat)
    back_part = lax.dot_general(
        flat_grad, w_down, contract_cols, preferred_element_type=jnp.float32
    ).astype(jnp.bfloat16)
    back_first = lax.psum(back_part, "dp")
    inputs_all, _ = lax.optimization_barrier((inputs.transpose(1, 0, 2), back_part))
    inputs_all = lax.all_gather(inputs_all, "tensor", axis=0, tiled=True).astype(jnp.float32)
    square_sum = lax.psum(jnp.sum(inputs_all * inputs_all, axis=2).T, "dp").T
    row_scale_all = lax.rsqrt(square_sum / full_width + epsilon)
    normed_all = (inputs_all * row_scale_all[:, :, None] * norm_gain).astype(jnp.bfloat16)
    row_scale = lax.dynamic_slice_in_dim(row_scale_all, start, local_rows, axis=0).T

    flat_normed = normed_all.reshape(rows * batches, local_feat)
    halvings = 3 - level_of_batch
    active = (tensor_index < jnp.right_shift(groups, halvings)).astype(jnp.float32)
    active_mask = jnp.tile(active, rows)[:, None]
    levels = jnp.arange(batches, dtype=jnp.int32)
    active_count = jnp.sum(
        (tensor_index < jnp.right_shift(groups, batches - 1 - levels)).astype(jnp.int32)
    )
    order = jnp.sum(
        jnp.where(level_of_batch[None, :] == batches - 1 - levels[:, None], levels[None, :], 0),
        axis=1,
    )

    def active_psum(count, pair):
        summed = lax.psum(tuple(part[:, :count] for part in pair), "dp")
        return tuple(
            jnp.pad(total, ((0, 0), (0, batches - count), (0, 0))) for total in summed
        )

    chunks = 1
    width = local_cols // chunks
    down_part = None
    normed_part = None
    hiddens, gate_grads, up_grads = [], [], []
    for chunk in range(chunks):
        cols = slice(chunk * width, (chunk + 1) * width)
        gate_w = w_gate[:, cols]
        up_w = w_up[:, cols]
        down_w = w_down[cols, :]
        gate_part = jnp.dot(flat_normed, gate_w, preferred_element_type=jnp.float32)
        up_part = jnp.dot(flat_normed, up_w, preferred_element_type=jnp.float32)
        parts = (gate_part.astype(jnp.bfloat16), up_part.astype(jnp.bfloat16))
        parts, back_sum = lax.optimization_barrier((parts, back_first))
        ranked = tuple(jnp.take(part.reshape(rows, batches, -1), order, axis=1) for part in parts)
        ranked = lax.switch(
            active_count - 1,
            [functools.partial(active_psum, count) for count in range(1, batches + 1)],
            ranked,
        )
        gate_sum, up_sum = (
            jnp.take(part, batches - 1 - level_of_batch, axis=1).reshape(rows * batches, -1)
            for part in ranked
        )
        hidden, gate_grad, up_grad = local_terms(
            gate_sum.astype(jnp.float32),
            up_sum.astype(jnp.float32),
            back_sum.astype(jnp.float32),
            active_mask,
        )
        hiddens.append(hidden)
        gate_grads.append(gate_grad)
        up_grads.append(up_grad)
        down_term = jnp.dot(hidden, down_w, preferred_element_type=jnp.float32)
        normed_term = lax.dot_general(
            gate_grad, gate_w, contract_cols, preferred_element_type=jnp.float32
        ) + lax.dot_general(up_grad, up_w, contract_cols, preferred_element_type=jnp.float32)
        down_part = down_term if down_part is None else down_part + down_term
        normed_part = normed_term if normed_part is None else normed_part + normed_term
    hidden = jnp.concatenate(hiddens, axis=1)
    gate_grad = jnp.concatenate(gate_grads, axis=1)
    up_grad = jnp.concatenate(up_grads, axis=1)

    stacked = jnp.stack(
        [
            down_part.reshape(rows, batches, local_feat),
            normed_part.reshape(rows, batches, local_feat),
        ],
        axis=1,
    ).astype(jnp.bfloat16)
    stacked = stacked.reshape(rows, 2 * batches, local_feat)
    scaled_all = (inputs_all * row_scale_all[:, :, None]).reshape(rows * batches, local_feat)
    gain_part = jnp.sum(normed_part * scaled_all, axis=0)
    row_all = jnp.sum(
        normed_part * (norm_gain * inputs_all.reshape(rows * batches, local_feat)), axis=1
    )
    reduced = lax.psum(jnp.concatenate([gain_part, row_all]), "tensor")
    d_gain = reduced[:local_feat]
    row_all = lax.psum(reduced[local_feat:], "dp").reshape(rows, batches)
    row_product = lax.dynamic_slice_in_dim(row_all, start, local_rows, axis=0).T
    hidden, flat_grad, _ = lax.optimization_barrier((hidden, flat_grad, stacked))
    shares = lax.psum_scatter(stacked, "tensor", scatter_dimension=0, tiled=True).astype(
        jnp.float32
    )
    shares = shares.reshape(local_rows, 2, batches, local_feat)
    down_output = shares[:, 0].transpose(1, 0, 2)
    normed_grad = shares[:, 1].transpose(1, 0, 2)

    down_out = lax.dot_general(
        hidden, flat_grad, contract_rows, preferred_element_type=jnp.float32
    ).astype(jnp.bfloat16)
    gate_out = lax.dot_general(
        flat_normed, gate_grad, contract_rows, preferred_element_type=jnp.float32
    ).astype(jnp.bfloat16)
    up_out = lax.dot_general(
        flat_normed, up_grad, contract_rows, preferred_element_type=jnp.float32
    ).astype(jnp.bfloat16)

    wide_grad = d_output.astype(jnp.float32)
    weighted = norm_gain * normed_grad
    outputs = (wide_inputs + down_output).astype(jnp.bfloat16)
    scale_cube = row_scale * row_scale * row_scale
    d_inputs = (
        wide_grad
        + row_scale[:, :, None] * weighted
        - wide_inputs * (scale_cube * row_product / full_width)[:, :, None]
    ).astype(jnp.bfloat16)
    return (outputs, d_inputs, d_gain, gate_out, up_out, down_out, row_product)


def solution(mesh):
    in_specs = (
        P(None, "tensor", "dp"),
        P("dp"),
        P("dp", "tensor"),
        P("dp", "tensor"),
        P("tensor", "dp"),
        P(None, "tensor", "dp"),
        P(),
    )
    out_specs = (
        P(None, "tensor", "dp"),
        P(None, "tensor", "dp"),
        P("dp"),
        P("dp", "tensor"),
        P("dp", "tensor"),
        P("tensor", "dp"),
        P(None, "tensor"),
    )
    return jax.shard_map(
        per_device, mesh=mesh, in_specs=in_specs, out_specs=out_specs, check_vma=False
    )
```

```python
import jax
import jax.numpy as jnp
from jax import lax
from jax.experimental import pallas as pl
from jax.sharding import PartitionSpec as P

epsilon = 1e-05
contract_cols = (((1,), (1,)), ((), ()))
contract_rows = (((0,), (0,)), ((), ()))


def local_terms(gate_sum, up_sum, back_sum, active_mask):
    sigmoid_gate = jax.nn.sigmoid(gate_sum)
    silu_gate = gate_sum * sigmoid_gate
    slope = sigmoid_gate * (1.0 + gate_sum * (1.0 - sigmoid_gate))
    hidden = (silu_gate * up_sum * active_mask).astype(jnp.bfloat16)
    gate_grad = (back_sum * up_sum * slope * active_mask).astype(jnp.bfloat16)
    up_grad = (back_sum * silu_gate * active_mask).astype(jnp.bfloat16)
    return (hidden, gate_grad, up_grad)


def back_kernel(grad_ref, weight_ref, out_ref):
    out_ref[...] = lax.dot_general(
        grad_ref[...], weight_ref[...], contract_cols, preferred_element_type=jnp.float32
    ).astype(out_ref.dtype)


def back_project(grad, weight):
    m, k = grad.shape
    n = weight.shape[0]
    tile = n // 4 if n % 512 == 0 else n
    return pl.pallas_call(
        back_kernel,
        grid=(n // tile,),
        in_specs=[
            pl.BlockSpec((m, k), lambda j: (0, 0)),
            pl.BlockSpec((tile, k), lambda j: (j, 0)),
        ],
        out_specs=pl.BlockSpec((m, tile), lambda j: (0, j)),
        out_shape=jax.ShapeDtypeStruct((m, n), jnp.bfloat16),
        cost_estimate=pl.CostEstimate(
            flops=2 * m * k * n, bytes_accessed=2 * (m * k + n * k + m * n), transcendentals=0
        ),
    )(grad, weight)


def per_device(inputs, norm_gain, w_gate, w_up, w_down, d_output, level_of_batch):
    groups = lax.axis_size("tensor")
    tensor_index = lax.axis_index("tensor")
    local_feat = w_gate.shape[0]
    local_cols = w_gate.shape[1]
    full_width = local_feat * lax.axis_size("dp")
    batches, local_rows, _ = inputs.shape
    wide_inputs = inputs.astype(jnp.float32)
    grad_all = lax.all_gather(d_output.transpose(1, 0, 2), "tensor", axis=0, tiled=True)
    rows = grad_all.shape[0]
    start = tensor_index * local_rows
    flat_grad = grad_all.reshape(rows * batches, local_feat)
    back_part = back_project(flat_grad, w_down)
    back_first = lax.psum(back_part, "dp")
    inputs_all, _ = lax.optimization_barrier((inputs.transpose(1, 0, 2), back_part))
    inputs_all = lax.all_gather(inputs_all, "tensor", axis=0, tiled=True).astype(jnp.float32)
    square_sum = lax.psum(jnp.sum(inputs_all * inputs_all, axis=2).T, "dp").T
    row_scale_all = lax.rsqrt(square_sum / full_width + epsilon)
    normed_all = (inputs_all * row_scale_all[:, :, None] * norm_gain).astype(jnp.bfloat16)
    row_scale = lax.dynamic_slice_in_dim(row_scale_all, start, local_rows, axis=0).T

    flat_normed = normed_all.reshape(rows * batches, local_feat)
    halvings = 3 - level_of_batch
    active = (tensor_index < jnp.right_shift(groups, halvings)).astype(jnp.float32)
    active_mask = jnp.tile(active, rows)[:, None]
    chunks = 1
    width = local_cols // chunks
    down_part = None
    normed_part = None
    hiddens, gate_grads, up_grads = [], [], []
    for chunk in range(chunks):
        cols = slice(chunk * width, (chunk + 1) * width)
        gate_w = w_gate[:, cols]
        up_w = w_up[:, cols]
        down_w = w_down[cols, :]
        gate_part = jnp.dot(flat_normed, gate_w, preferred_element_type=jnp.float32)
        up_part = jnp.dot(flat_normed, up_w, preferred_element_type=jnp.float32)
        parts = (gate_part.astype(jnp.bfloat16), up_part.astype(jnp.bfloat16))
        parts, back_sum = lax.optimization_barrier((parts, back_first))
        gate_sum, up_sum = lax.psum(parts, "dp")
        hidden, gate_grad, up_grad = local_terms(
            gate_sum.astype(jnp.float32),
            up_sum.astype(jnp.float32),
            back_sum.astype(jnp.float32),
            active_mask,
        )
        hiddens.append(hidden)
        gate_grads.append(gate_grad)
        up_grads.append(up_grad)
        down_term = jnp.dot(hidden, down_w, preferred_element_type=jnp.float32)
        normed_term = lax.dot_general(
            gate_grad, gate_w, contract_cols, preferred_element_type=jnp.float32
        ) + lax.dot_general(up_grad, up_w, contract_cols, preferred_element_type=jnp.float32)
        down_part = down_term if down_part is None else down_part + down_term
        normed_part = normed_term if normed_part is None else normed_part + normed_term
    hidden = jnp.concatenate(hiddens, axis=1)
    gate_grad = jnp.concatenate(gate_grads, axis=1)
    up_grad = jnp.concatenate(up_grads, axis=1)

    stacked = jnp.stack(
        [
            down_part.reshape(rows, batches, local_feat),
            normed_part.reshape(rows, batches, local_feat),
        ],
        axis=1,
    ).astype(jnp.bfloat16)
    stacked = stacked.reshape(rows, 2 * batches, local_feat)
    scaled_all = (inputs_all * row_scale_all[:, :, None]).reshape(rows * batches, local_feat)
    gain_part = jnp.sum(normed_part * scaled_all, axis=0)
    row_all = jnp.sum(
        normed_part * (norm_gain * inputs_all.reshape(rows * batches, local_feat)), axis=1
    )
    reduced = lax.psum(jnp.concatenate([gain_part, row_all]), "tensor")
    d_gain = reduced[:local_feat]
    row_all = lax.psum(reduced[local_feat:], "dp").reshape(rows, batches)
    row_product = lax.dynamic_slice_in_dim(row_all, start, local_rows, axis=0).T
    hidden, flat_grad, _ = lax.optimization_barrier((hidden, flat_grad, stacked))
    shares = lax.psum_scatter(stacked, "tensor", scatter_dimension=0, tiled=True).astype(
        jnp.float32
    )
    shares = shares.reshape(local_rows, 2, batches, local_feat)
    down_output = shares[:, 0].transpose(1, 0, 2)
    normed_grad = shares[:, 1].transpose(1, 0, 2)

    down_out = lax.dot_general(
        hidden, flat_grad, contract_rows, preferred_element_type=jnp.float32
    ).astype(jnp.bfloat16)
    gate_out = lax.dot_general(
        flat_normed, gate_grad, contract_rows, preferred_element_type=jnp.float32
    ).astype(jnp.bfloat16)
    up_out = lax.dot_general(
        flat_normed, up_grad, contract_rows, preferred_element_type=jnp.float32
    ).astype(jnp.bfloat16)

    wide_grad = d_output.astype(jnp.float32)
    weighted = norm_gain * normed_grad
    outputs = (wide_inputs + down_output).astype(jnp.bfloat16)
    scale_cube = row_scale * row_scale * row_scale
    d_inputs = (
        wide_grad
        + row_scale[:, :, None] * weighted
        - wide_inputs * (scale_cube * row_product / full_width)[:, :, None]
    ).astype(jnp.bfloat16)
    return (outputs, d_inputs, d_gain, gate_out, up_out, down_out, row_product)


def solution(mesh):
    in_specs = (
        P(None, "tensor", "dp"),
        P("dp"),
        P("dp", "tensor"),
        P("dp", "tensor"),
        P("tensor", "dp"),
        P(None, "tensor", "dp"),
        P(),
    )
    out_specs = (
        P(None, "tensor", "dp"),
        P(None, "tensor", "dp"),
        P("dp"),
        P("dp", "tensor"),
        P("dp", "tensor"),
        P("tensor", "dp"),
        P(None, "tensor"),
    )
    return jax.shard_map(
        per_device, mesh=mesh, in_specs=in_specs, out_specs=out_specs, check_vma=False
    )
```

```python
import jax
import jax.numpy as jnp
from jax import lax
from jax.experimental import pallas as pl
from jax.sharding import PartitionSpec as P

epsilon = 1e-05
contract_cols = (((1,), (1,)), ((), ()))
contract_rows = (((0,), (0,)), ((), ()))


def local_terms(gate_sum, up_sum, back_sum, active_mask):
    sigmoid_gate = jax.nn.sigmoid(gate_sum)
    silu_gate = gate_sum * sigmoid_gate
    slope = sigmoid_gate * (1.0 + gate_sum * (1.0 - sigmoid_gate))
    hidden = (silu_gate * up_sum * active_mask).astype(jnp.bfloat16)
    gate_grad = (back_sum * up_sum * slope * active_mask).astype(jnp.bfloat16)
    up_grad = (back_sum * silu_gate * active_mask).astype(jnp.bfloat16)
    return (hidden, gate_grad, up_grad)


def back_kernel(grad_ref, weight_ref, out_ref):
    out_ref[...] = lax.dot_general(
        grad_ref[...], weight_ref[...], contract_cols, preferred_element_type=jnp.float32
    ).astype(out_ref.dtype)


def back_project(grad, weight):
    m, k = grad.shape
    n = weight.shape[0]
    tile = n // 4 if n % 512 == 0 else n
    return pl.pallas_call(
        back_kernel,
        grid=(n // tile,),
        in_specs=[
            pl.BlockSpec((m, k), lambda j: (0, 0)),
            pl.BlockSpec((tile, k), lambda j: (j, 0)),
        ],
        out_specs=pl.BlockSpec((m, tile), lambda j: (0, j)),
        out_shape=jax.ShapeDtypeStruct((m, n), jnp.bfloat16),
        cost_estimate=pl.CostEstimate(
            flops=2 * m * k * n, bytes_accessed=2 * (m * k + n * k + m * n), transcendentals=0
        ),
    )(grad, weight)


def per_device(inputs, norm_gain, w_gate, w_up, w_down, d_output, level_of_batch):
    groups = lax.axis_size("tensor")
    tensor_index = lax.axis_index("tensor")
    local_feat = w_gate.shape[0]
    local_cols = w_gate.shape[1]
    full_width = local_feat * lax.axis_size("dp")
    batches, local_rows, _ = inputs.shape
    wide_inputs = inputs.astype(jnp.float32)
    grad_all = lax.all_gather(d_output.transpose(1, 0, 2), "tensor", axis=0, tiled=True)
    rows = grad_all.shape[0]
    start = tensor_index * local_rows
    flat_grad = grad_all.reshape(rows * batches, local_feat)
    back_part = back_project(flat_grad, w_down)
    back_first = lax.psum(back_part, "dp")
    inputs_all, _ = lax.optimization_barrier((inputs.transpose(1, 0, 2), back_part))
    inputs_all = lax.all_gather(inputs_all, "tensor", axis=0, tiled=True).astype(jnp.float32)
    square_sum = lax.psum(jnp.sum(inputs_all * inputs_all, axis=2).T, "dp").T
    row_scale_all = lax.rsqrt(square_sum / full_width + epsilon)
    normed_all = (inputs_all * row_scale_all[:, :, None] * norm_gain).astype(jnp.bfloat16)
    row_scale = lax.dynamic_slice_in_dim(row_scale_all, start, local_rows, axis=0).T

    flat_normed = normed_all.reshape(rows * batches, local_feat)
    halvings = 3 - level_of_batch
    active = (tensor_index < jnp.right_shift(groups, halvings)).astype(jnp.float32)
    active_mask = jnp.tile(active, rows)[:, None]
    chunks = 1
    width = local_cols // chunks
    down_part = None
    normed_part = None
    hiddens, gate_grads, up_grads = [], [], []
    for chunk in range(chunks):
        cols = slice(chunk * width, (chunk + 1) * width)
        gate_w = w_gate[:, cols]
        up_w = w_up[:, cols]
        down_w = w_down[cols, :]
        gate_part = jnp.dot(flat_normed, gate_w, preferred_element_type=jnp.float32)
        up_part = jnp.dot(flat_normed, up_w, preferred_element_type=jnp.float32)
        parts = (gate_part.astype(jnp.bfloat16), up_part.astype(jnp.bfloat16))
        parts, back_sum = lax.optimization_barrier((parts, back_first))
        gate_sum, up_sum = lax.psum(parts, "dp")
        hidden, gate_grad, up_grad = local_terms(
            gate_sum.astype(jnp.float32),
            up_sum.astype(jnp.float32),
            back_sum.astype(jnp.float32),
            active_mask,
        )
        hiddens.append(hidden)
        gate_grads.append(gate_grad)
        up_grads.append(up_grad)
        down_term = jnp.dot(hidden, down_w, preferred_element_type=jnp.float32)
        normed_term = lax.dot_general(
            gate_grad, gate_w, contract_cols, preferred_element_type=jnp.float32
        ) + lax.dot_general(up_grad, up_w, contract_cols, preferred_element_type=jnp.float32)
        down_part = down_term if down_part is None else down_part + down_term
        normed_part = normed_term if normed_part is None else normed_part + normed_term
    hidden = jnp.concatenate(hiddens, axis=1)
    gate_grad = jnp.concatenate(gate_grads, axis=1)
    up_grad = jnp.concatenate(up_grads, axis=1)

    stacked = jnp.concatenate(
        [down_part.astype(jnp.bfloat16), normed_part.astype(jnp.bfloat16)], axis=1
    ).reshape(rows, 2 * batches, local_feat)
    scaled_all = (inputs_all * row_scale_all[:, :, None]).reshape(rows * batches, local_feat)
    gain_part = jnp.sum(normed_part * scaled_all, axis=0)
    row_all = jnp.sum(
        normed_part * (norm_gain * inputs_all.reshape(rows * batches, local_feat)), axis=1
    )
    reduced = lax.psum(jnp.concatenate([gain_part, row_all]), "tensor")
    d_gain = reduced[:local_feat]
    row_all = lax.psum(reduced[local_feat:], "dp").reshape(rows, batches)
    row_product = lax.dynamic_slice_in_dim(row_all, start, local_rows, axis=0).T
    hidden, flat_grad, _ = lax.optimization_barrier((hidden, flat_grad, stacked))
    shares = lax.psum_scatter(stacked, "tensor", scatter_dimension=0, tiled=True).astype(
        jnp.float32
    )
    shares = shares.reshape(local_rows, batches, 2, local_feat)
    down_output = shares[:, :, 0].transpose(1, 0, 2)
    normed_grad = shares[:, :, 1].transpose(1, 0, 2)

    down_out = lax.dot_general(
        hidden, flat_grad, contract_rows, preferred_element_type=jnp.float32
    ).astype(jnp.bfloat16)
    gate_out = lax.dot_general(
        flat_normed, gate_grad, contract_rows, preferred_element_type=jnp.float32
    ).astype(jnp.bfloat16)
    up_out = lax.dot_general(
        flat_normed, up_grad, contract_rows, preferred_element_type=jnp.float32
    ).astype(jnp.bfloat16)

    wide_grad = d_output.astype(jnp.float32)
    weighted = norm_gain * normed_grad
    outputs = (wide_inputs + down_output).astype(jnp.bfloat16)
    scale_cube = row_scale * row_scale * row_scale
    d_inputs = (
        wide_grad
        + row_scale[:, :, None] * weighted
        - wide_inputs * (scale_cube * row_product / full_width)[:, :, None]
    ).astype(jnp.bfloat16)
    return (outputs, d_inputs, d_gain, gate_out, up_out, down_out, row_product)


def solution(mesh):
    in_specs = (
        P(None, "tensor", "dp"),
        P("dp"),
        P("dp", "tensor"),
        P("dp", "tensor"),
        P("tensor", "dp"),
        P(None, "tensor", "dp"),
        P(),
    )
    out_specs = (
        P(None, "tensor", "dp"),
        P(None, "tensor", "dp"),
        P("dp"),
        P("dp", "tensor"),
        P("dp", "tensor"),
        P("tensor", "dp"),
        P(None, "tensor"),
    )
    return jax.shard_map(
        per_device, mesh=mesh, in_specs=in_specs, out_specs=out_specs, check_vma=False
    )
```

```python
import jax
import jax.numpy as jnp
from jax import lax
from jax.experimental import pallas as pl
from jax.sharding import PartitionSpec as P

epsilon = 1e-05
contract_cols = (((1,), (1,)), ((), ()))
contract_rows = (((0,), (0,)), ((), ()))


def local_terms(gate_sum, up_sum, back_sum, active_mask):
    sigmoid_gate = jax.nn.sigmoid(gate_sum)
    silu_gate = gate_sum * sigmoid_gate
    slope = sigmoid_gate * (1.0 + gate_sum * (1.0 - sigmoid_gate))
    hidden = (silu_gate * up_sum * active_mask).astype(jnp.bfloat16)
    gate_grad = (back_sum * up_sum * slope * active_mask).astype(jnp.bfloat16)
    up_grad = (back_sum * silu_gate * active_mask).astype(jnp.bfloat16)
    return (hidden, gate_grad, up_grad)


def back_kernel(grad_ref, weight_ref, out_ref):
    out_ref[...] = lax.dot_general(
        grad_ref[...], weight_ref[...], contract_cols, preferred_element_type=jnp.float32
    ).astype(out_ref.dtype)


def back_project(grad, weight):
    m, k = grad.shape
    n = weight.shape[0]
    tile = n // 4 if n % 512 == 0 else n
    return pl.pallas_call(
        back_kernel,
        grid=(n // tile,),
        in_specs=[
            pl.BlockSpec((m, k), lambda j: (0, 0)),
            pl.BlockSpec((tile, k), lambda j: (j, 0)),
        ],
        out_specs=pl.BlockSpec((m, tile), lambda j: (0, j)),
        out_shape=jax.ShapeDtypeStruct((m, n), jnp.bfloat16),
        cost_estimate=pl.CostEstimate(
            flops=2 * m * k * n, bytes_accessed=2 * (m * k + n * k + m * n), transcendentals=0
        ),
    )(grad, weight)


def per_device(inputs, norm_gain, w_gate, w_up, w_down, d_output, level_of_batch):
    groups = lax.axis_size("tensor")
    tensor_index = lax.axis_index("tensor")
    local_feat = w_gate.shape[0]
    local_cols = w_gate.shape[1]
    full_width = local_feat * lax.axis_size("dp")
    batches, local_rows, _ = inputs.shape
    wide_inputs = inputs.astype(jnp.float32)
    grad_all = lax.all_gather(d_output, "tensor", axis=1, tiled=True)
    rows = grad_all.shape[1]
    start = tensor_index * local_rows
    flat_grad = grad_all.reshape(rows * batches, local_feat)
    back_part = back_project(flat_grad, w_down)
    back_first = lax.psum(back_part, "dp")
    inputs_all, _ = lax.optimization_barrier((inputs, back_part))
    inputs_all = lax.all_gather(inputs_all, "tensor", axis=1, tiled=True).astype(jnp.float32)
    square_sum = lax.psum(jnp.sum(inputs_all * inputs_all, axis=2), "dp")
    row_scale_all = lax.rsqrt(square_sum / full_width + epsilon)
    normed_all = (inputs_all * row_scale_all[:, :, None] * norm_gain).astype(jnp.bfloat16)
    row_scale = lax.dynamic_slice_in_dim(row_scale_all, start, local_rows, axis=1)

    flat_normed = normed_all.reshape(rows * batches, local_feat)
    halvings = 3 - level_of_batch
    active = (tensor_index < jnp.right_shift(groups, halvings)).astype(jnp.float32)
    active_mask = jnp.repeat(active, rows)[:, None]
    chunks = 1
    width = local_cols // chunks
    down_part = None
    normed_part = None
    hiddens, gate_grads, up_grads = [], [], []
    for chunk in range(chunks):
        cols = slice(chunk * width, (chunk + 1) * width)
        gate_w = w_gate[:, cols]
        up_w = w_up[:, cols]
        down_w = w_down[cols, :]
        gate_part = jnp.dot(flat_normed, gate_w, preferred_element_type=jnp.float32)
        up_part = jnp.dot(flat_normed, up_w, preferred_element_type=jnp.float32)
        parts = (gate_part.astype(jnp.bfloat16), up_part.astype(jnp.bfloat16))
        parts, back_sum = lax.optimization_barrier((parts, back_first))
        gate_sum, up_sum = lax.psum(parts, "dp")
        hidden, gate_grad, up_grad = local_terms(
            gate_sum.astype(jnp.float32),
            up_sum.astype(jnp.float32),
            back_sum.astype(jnp.float32),
            active_mask,
        )
        hiddens.append(hidden)
        gate_grads.append(gate_grad)
        up_grads.append(up_grad)
        down_term = jnp.dot(hidden, down_w, preferred_element_type=jnp.float32)
        normed_term = lax.dot_general(
            gate_grad, gate_w, contract_cols, preferred_element_type=jnp.float32
        ) + lax.dot_general(up_grad, up_w, contract_cols, preferred_element_type=jnp.float32)
        down_part = down_term if down_part is None else down_part + down_term
        normed_part = normed_term if normed_part is None else normed_part + normed_term
    hidden = jnp.concatenate(hiddens, axis=1)
    gate_grad = jnp.concatenate(gate_grads, axis=1)
    up_grad = jnp.concatenate(up_grads, axis=1)

    stacked = jnp.concatenate(
        [down_part.astype(jnp.bfloat16), normed_part.astype(jnp.bfloat16)], axis=1
    ).reshape(batches, rows, 2 * local_feat)
    stacked = stacked.transpose(1, 0, 2).reshape(rows, 2 * batches, local_feat)
    scaled_all = (inputs_all * row_scale_all[:, :, None]).reshape(rows * batches, local_feat)
    gain_part = jnp.sum(normed_part * scaled_all, axis=0)
    row_all = jnp.sum(
        normed_part * (norm_gain * inputs_all.reshape(rows * batches, local_feat)), axis=1
    )
    reduced = lax.psum(jnp.concatenate([gain_part, row_all]), "tensor")
    d_gain = reduced[:local_feat]
    row_all = lax.psum(reduced[local_feat:], "dp").reshape(batches, rows)
    row_product = lax.dynamic_slice_in_dim(row_all, start, local_rows, axis=1)
    hidden, flat_grad, _ = lax.optimization_barrier((hidden, flat_grad, stacked))
    shares = lax.psum_scatter(stacked, "tensor", scatter_dimension=0, tiled=True).astype(
        jnp.float32
    )
    shares = shares.reshape(local_rows, batches, 2, local_feat)
    down_output = shares[:, :, 0].transpose(1, 0, 2)
    normed_grad = shares[:, :, 1].transpose(1, 0, 2)

    down_out = lax.dot_general(
        hidden, flat_grad, contract_rows, preferred_element_type=jnp.float32
    ).astype(jnp.bfloat16)
    gate_out = lax.dot_general(
        flat_normed, gate_grad, contract_rows, preferred_element_type=jnp.float32
    ).astype(jnp.bfloat16)
    up_out = lax.dot_general(
        flat_normed, up_grad, contract_rows, preferred_element_type=jnp.float32
    ).astype(jnp.bfloat16)

    wide_grad = d_output.astype(jnp.float32)
    weighted = norm_gain * normed_grad
    outputs = (wide_inputs + down_output).astype(jnp.bfloat16)
    scale_cube = row_scale * row_scale * row_scale
    d_inputs = (
        wide_grad
        + row_scale[:, :, None] * weighted
        - wide_inputs * (scale_cube * row_product / full_width)[:, :, None]
    ).astype(jnp.bfloat16)
    return (outputs, d_inputs, d_gain, gate_out, up_out, down_out, row_product)


def solution(mesh):
    in_specs = (
        P(None, "tensor", "dp"),
        P("dp"),
        P("dp", "tensor"),
        P("dp", "tensor"),
        P("tensor", "dp"),
        P(None, "tensor", "dp"),
        P(),
    )
    out_specs = (
        P(None, "tensor", "dp"),
        P(None, "tensor", "dp"),
        P("dp"),
        P("dp", "tensor"),
        P("dp", "tensor"),
        P("tensor", "dp"),
        P(None, "tensor"),
    )
    return jax.shard_map(
        per_device, mesh=mesh, in_specs=in_specs, out_specs=out_specs, check_vma=False
    )
```

```python
import jax
import jax.numpy as jnp
from jax import lax
from jax.experimental import pallas as pl
from jax.sharding import PartitionSpec as P

epsilon = 1e-05
contract_cols = (((1,), (1,)), ((), ()))
contract_rows = (((0,), (0,)), ((), ()))


def local_terms(gate_sum, up_sum, back_sum, active_mask):
    sigmoid_gate = jax.nn.sigmoid(gate_sum)
    silu_gate = gate_sum * sigmoid_gate
    slope = sigmoid_gate * (1.0 + gate_sum * (1.0 - sigmoid_gate))
    hidden = (silu_gate * up_sum * active_mask).astype(jnp.bfloat16)
    gate_grad = (back_sum * up_sum * slope * active_mask).astype(jnp.bfloat16)
    up_grad = (back_sum * silu_gate * active_mask).astype(jnp.bfloat16)
    return (hidden, gate_grad, up_grad)


def back_kernel(grad_ref, weight_ref, out_ref):
    out_ref[...] = lax.dot_general(
        grad_ref[...], weight_ref[...], contract_cols, preferred_element_type=jnp.float32
    ).astype(out_ref.dtype)


def back_project(grad, weight):
    m, k = grad.shape
    n = weight.shape[0]
    tile = n // 4 if n % 512 == 0 else n
    return pl.pallas_call(
        back_kernel,
        grid=(n // tile,),
        in_specs=[
            pl.BlockSpec((m, k), lambda j: (0, 0)),
            pl.BlockSpec((tile, k), lambda j: (j, 0)),
        ],
        out_specs=pl.BlockSpec((m, tile), lambda j: (0, j)),
        out_shape=jax.ShapeDtypeStruct((m, n), jnp.bfloat16),
        cost_estimate=pl.CostEstimate(
            flops=2 * m * k * n, bytes_accessed=2 * (m * k + n * k + m * n), transcendentals=0
        ),
    )(grad, weight)


def per_device(inputs, norm_gain, w_gate, w_up, w_down, d_output, level_of_batch):
    groups = lax.axis_size("tensor")
    tensor_index = lax.axis_index("tensor")
    local_feat = w_gate.shape[0]
    local_cols = w_gate.shape[1]
    full_width = local_feat * lax.axis_size("dp")
    batches, local_rows, _ = inputs.shape
    wide_inputs = inputs.astype(jnp.float32)
    grad_all = lax.all_gather(d_output, "tensor", axis=1, tiled=True)
    rows = grad_all.shape[1]
    start = tensor_index * local_rows
    flat_grad = grad_all.reshape(rows * batches, local_feat)
    back_part = back_project(flat_grad, w_down)
    back_first = lax.psum(back_part, "dp")
    inputs_all, _ = lax.optimization_barrier((inputs, back_part))
    inputs_all = lax.all_gather(inputs_all, "tensor", axis=1, tiled=True).astype(jnp.float32)
    square_sum = lax.psum(jnp.sum(inputs_all * inputs_all, axis=2), "dp")
    row_scale_all = lax.rsqrt(square_sum / full_width + epsilon)
    normed_all = (inputs_all * row_scale_all[:, :, None] * norm_gain).astype(jnp.bfloat16)
    row_scale = lax.dynamic_slice_in_dim(row_scale_all, start, local_rows, axis=1)

    flat_normed = normed_all.reshape(rows * batches, local_feat)
    halvings = 3 - level_of_batch
    active = (tensor_index < jnp.right_shift(groups, halvings)).astype(jnp.float32)
    active_mask = jnp.repeat(active, rows)[:, None]
    chunks = 1
    width = local_cols // chunks
    down_part = None
    normed_part = None
    hiddens, gate_grads, up_grads = [], [], []
    for chunk in range(chunks):
        cols = slice(chunk * width, (chunk + 1) * width)
        gate_w = w_gate[:, cols]
        up_w = w_up[:, cols]
        down_w = w_down[cols, :]
        gate_part = jnp.dot(flat_normed, gate_w, preferred_element_type=jnp.float32)
        up_part = jnp.dot(flat_normed, up_w, preferred_element_type=jnp.float32)
        parts = (gate_part.astype(jnp.bfloat16), up_part.astype(jnp.bfloat16))
        parts, back_sum = lax.optimization_barrier((parts, back_first))
        gate_sum, up_sum = lax.psum(parts, "dp")
        hidden, gate_grad, up_grad = local_terms(
            gate_sum.astype(jnp.float32),
            up_sum.astype(jnp.float32),
            back_sum.astype(jnp.float32),
            active_mask,
        )
        hiddens.append(hidden)
        gate_grads.append(gate_grad)
        up_grads.append(up_grad)
        down_term = jnp.dot(hidden, down_w, preferred_element_type=jnp.float32)
        normed_term = lax.dot_general(
            gate_grad, gate_w, contract_cols, preferred_element_type=jnp.float32
        ) + lax.dot_general(up_grad, up_w, contract_cols, preferred_element_type=jnp.float32)
        down_part = down_term if down_part is None else down_part + down_term
        normed_part = normed_term if normed_part is None else normed_part + normed_term
    hidden = jnp.concatenate(hiddens, axis=1)
    gate_grad = jnp.concatenate(gate_grads, axis=1)
    up_grad = jnp.concatenate(up_grads, axis=1)

    stacked = jnp.concatenate(
        [down_part.astype(jnp.bfloat16), normed_part.astype(jnp.bfloat16)], axis=1
    ).reshape(batches, rows, 2 * local_feat)
    stacked = stacked.transpose(1, 0, 2).reshape(rows, 2 * batches, local_feat)
    scaled_all = (inputs_all * row_scale_all[:, :, None]).reshape(rows * batches, local_feat)
    gain_part = jnp.sum(normed_part * scaled_all, axis=0)
    row_all = jnp.sum(
        normed_part * (norm_gain * inputs_all.reshape(rows * batches, local_feat)), axis=1
    )
    reduced = jnp.sum(
        lax.all_gather(jnp.concatenate([gain_part, row_all]), "tensor", axis=0), axis=0
    )
    d_gain = reduced[:local_feat]
    row_all = jnp.sum(lax.all_gather(reduced[local_feat:], "dp", axis=0), axis=0)
    row_all = row_all.reshape(batches, rows)
    row_product = lax.dynamic_slice_in_dim(row_all, start, local_rows, axis=1)
    hidden, flat_grad, _ = lax.optimization_barrier((hidden, flat_grad, stacked))
    shares = lax.psum_scatter(stacked, "tensor", scatter_dimension=0, tiled=True).astype(
        jnp.float32
    )
    shares = shares.reshape(local_rows, batches, 2, local_feat)
    down_output = shares[:, :, 0].transpose(1, 0, 2)
    normed_grad = shares[:, :, 1].transpose(1, 0, 2)

    down_out = lax.dot_general(
        hidden, flat_grad, contract_rows, preferred_element_type=jnp.float32
    ).astype(jnp.bfloat16)
    gate_out = lax.dot_general(
        flat_normed, gate_grad, contract_rows, preferred_element_type=jnp.float32
    ).astype(jnp.bfloat16)
    up_out = lax.dot_general(
        flat_normed, up_grad, contract_rows, preferred_element_type=jnp.float32
    ).astype(jnp.bfloat16)

    wide_grad = d_output.astype(jnp.float32)
    weighted = norm_gain * normed_grad
    outputs = (wide_inputs + down_output).astype(jnp.bfloat16)
    scale_cube = row_scale * row_scale * row_scale
    d_inputs = (
        wide_grad
        + row_scale[:, :, None] * weighted
        - wide_inputs * (scale_cube * row_product / full_width)[:, :, None]
    ).astype(jnp.bfloat16)
    return (outputs, d_inputs, d_gain, gate_out, up_out, down_out, row_product)


def solution(mesh):
    in_specs = (
        P(None, "tensor", "dp"),
        P("dp"),
        P("dp", "tensor"),
        P("dp", "tensor"),
        P("tensor", "dp"),
        P(None, "tensor", "dp"),
        P(),
    )
    out_specs = (
        P(None, "tensor", "dp"),
        P(None, "tensor", "dp"),
        P("dp"),
        P("dp", "tensor"),
        P("dp", "tensor"),
        P("tensor", "dp"),
        P(None, "tensor"),
    )
    return jax.shard_map(
        per_device, mesh=mesh, in_specs=in_specs, out_specs=out_specs, check_vma=False
    )
```

```python
import jax
import jax.numpy as jnp
from jax import lax
from jax.experimental import pallas as pl
from jax.sharding import PartitionSpec as P

epsilon = 1e-05
contract_cols = (((1,), (1,)), ((), ()))
contract_rows = (((0,), (0,)), ((), ()))


def local_terms(gate_sum, up_sum, back_sum, active_mask):
    sigmoid_gate = jax.nn.sigmoid(gate_sum)
    silu_gate = gate_sum * sigmoid_gate
    slope = sigmoid_gate * (1.0 + gate_sum * (1.0 - sigmoid_gate))
    hidden = (silu_gate * up_sum * active_mask).astype(jnp.bfloat16)
    gate_grad = (back_sum * up_sum * slope * active_mask).astype(jnp.bfloat16)
    up_grad = (back_sum * silu_gate * active_mask).astype(jnp.bfloat16)
    return (hidden, gate_grad, up_grad)


def back_kernel(grad_ref, weight_ref, out_ref):
    out_ref[...] = lax.dot_general(
        grad_ref[...], weight_ref[...], contract_cols, preferred_element_type=jnp.float32
    ).astype(out_ref.dtype)


def back_project(grad, weight):
    m, k = grad.shape
    n = weight.shape[0]
    tile = n // 4 if n % 512 == 0 else n
    return pl.pallas_call(
        back_kernel,
        grid=(n // tile,),
        in_specs=[
            pl.BlockSpec((m, k), lambda j: (0, 0)),
            pl.BlockSpec((tile, k), lambda j: (j, 0)),
        ],
        out_specs=pl.BlockSpec((m, tile), lambda j: (0, j)),
        out_shape=jax.ShapeDtypeStruct((m, n), jnp.bfloat16),
        cost_estimate=pl.CostEstimate(
            flops=2 * m * k * n, bytes_accessed=2 * (m * k + n * k + m * n), transcendentals=0
        ),
    )(grad, weight)


def per_device(inputs, norm_gain, w_gate, w_up, w_down, d_output, level_of_batch):
    groups = lax.axis_size("tensor")
    tensor_index = lax.axis_index("tensor")
    local_feat = w_gate.shape[0]
    local_cols = w_gate.shape[1]
    full_width = local_feat * lax.axis_size("dp")
    batches, local_rows, _ = inputs.shape
    wide_inputs = inputs.astype(jnp.float32)
    grad_all = lax.all_gather(d_output, "tensor", axis=1, tiled=True)
    rows = grad_all.shape[1]
    start = tensor_index * local_rows
    flat_grad = grad_all.reshape(rows * batches, local_feat)
    back_part = back_project(flat_grad, w_down)
    back_first = lax.psum(back_part, "dp")
    inputs_all, _ = lax.optimization_barrier((inputs, back_part))
    inputs_all = lax.all_gather(inputs_all, "tensor", axis=1, tiled=True).astype(jnp.float32)
    square_sum = jnp.sum(
        lax.all_gather(jnp.sum(inputs_all * inputs_all, axis=2), "dp", axis=0), axis=0
    )
    row_scale_all = lax.rsqrt(square_sum / full_width + epsilon)
    normed_all = (inputs_all * row_scale_all[:, :, None] * norm_gain).astype(jnp.bfloat16)
    row_scale = lax.dynamic_slice_in_dim(row_scale_all, start, local_rows, axis=1)

    flat_normed = normed_all.reshape(rows * batches, local_feat)
    halvings = 3 - level_of_batch
    active = (tensor_index < jnp.right_shift(groups, halvings)).astype(jnp.float32)
    active_mask = jnp.repeat(active, rows)[:, None]
    chunks = 1
    width = local_cols // chunks
    down_part = None
    normed_part = None
    hiddens, gate_grads, up_grads = [], [], []
    for chunk in range(chunks):
        cols = slice(chunk * width, (chunk + 1) * width)
        gate_w = w_gate[:, cols]
        up_w = w_up[:, cols]
        down_w = w_down[cols, :]
        gate_part = jnp.dot(flat_normed, gate_w, preferred_element_type=jnp.float32)
        up_part = jnp.dot(flat_normed, up_w, preferred_element_type=jnp.float32)
        parts = (gate_part.astype(jnp.bfloat16), up_part.astype(jnp.bfloat16))
        parts, back_sum = lax.optimization_barrier((parts, back_first))
        gate_sum, up_sum = lax.psum(parts, "dp")
        hidden, gate_grad, up_grad = local_terms(
            gate_sum.astype(jnp.float32),
            up_sum.astype(jnp.float32),
            back_sum.astype(jnp.float32),
            active_mask,
        )
        hiddens.append(hidden)
        gate_grads.append(gate_grad)
        up_grads.append(up_grad)
        down_term = jnp.dot(hidden, down_w, preferred_element_type=jnp.float32)
        normed_term = lax.dot_general(
            gate_grad, gate_w, contract_cols, preferred_element_type=jnp.float32
        ) + lax.dot_general(up_grad, up_w, contract_cols, preferred_element_type=jnp.float32)
        down_part = down_term if down_part is None else down_part + down_term
        normed_part = normed_term if normed_part is None else normed_part + normed_term
    hidden = jnp.concatenate(hiddens, axis=1)
    gate_grad = jnp.concatenate(gate_grads, axis=1)
    up_grad = jnp.concatenate(up_grads, axis=1)

    stacked = jnp.concatenate(
        [down_part.astype(jnp.bfloat16), normed_part.astype(jnp.bfloat16)], axis=1
    ).reshape(batches, rows, 2 * local_feat)
    stacked = stacked.transpose(1, 0, 2).reshape(rows, 2 * batches, local_feat)
    scaled_all = (inputs_all * row_scale_all[:, :, None]).reshape(rows * batches, local_feat)
    gain_part = jnp.sum(normed_part * scaled_all, axis=0)
    row_all = jnp.sum(
        normed_part * (norm_gain * inputs_all.reshape(rows * batches, local_feat)), axis=1
    )
    reduced = jnp.sum(
        lax.all_gather(jnp.concatenate([gain_part, row_all]), "tensor", axis=0), axis=0
    )
    d_gain = reduced[:local_feat]
    row_all = jnp.sum(lax.all_gather(reduced[local_feat:], "dp", axis=0), axis=0)
    row_all = row_all.reshape(batches, rows)
    row_product = lax.dynamic_slice_in_dim(row_all, start, local_rows, axis=1)
    hidden, flat_grad, _ = lax.optimization_barrier((hidden, flat_grad, stacked))
    shares = lax.psum_scatter(stacked, "tensor", scatter_dimension=0, tiled=True).astype(
        jnp.float32
    )
    shares = shares.reshape(local_rows, batches, 2, local_feat)
    down_output = shares[:, :, 0].transpose(1, 0, 2)
    normed_grad = shares[:, :, 1].transpose(1, 0, 2)

    down_out = lax.dot_general(
        hidden, flat_grad, contract_rows, preferred_element_type=jnp.float32
    ).astype(jnp.bfloat16)
    gate_out = lax.dot_general(
        flat_normed, gate_grad, contract_rows, preferred_element_type=jnp.float32
    ).astype(jnp.bfloat16)
    up_out = lax.dot_general(
        flat_normed, up_grad, contract_rows, preferred_element_type=jnp.float32
    ).astype(jnp.bfloat16)

    wide_grad = d_output.astype(jnp.float32)
    weighted = norm_gain * normed_grad
    outputs = (wide_inputs + down_output).astype(jnp.bfloat16)
    scale_cube = row_scale * row_scale * row_scale
    d_inputs = (
        wide_grad
        + row_scale[:, :, None] * weighted
        - wide_inputs * (scale_cube * row_product / full_width)[:, :, None]
    ).astype(jnp.bfloat16)
    return (outputs, d_inputs, d_gain, gate_out, up_out, down_out, row_product)


def solution(mesh):
    in_specs = (
        P(None, "tensor", "dp"),
        P("dp"),
        P("dp", "tensor"),
        P("dp", "tensor"),
        P("tensor", "dp"),
        P(None, "tensor", "dp"),
        P(),
    )
    out_specs = (
        P(None, "tensor", "dp"),
        P(None, "tensor", "dp"),
        P("dp"),
        P("dp", "tensor"),
        P("dp", "tensor"),
        P("tensor", "dp"),
        P(None, "tensor"),
    )
    return jax.shard_map(
        per_device, mesh=mesh, in_specs=in_specs, out_specs=out_specs, check_vma=False
    )
```

```python
import jax
import jax.numpy as jnp
from jax import lax
from jax.experimental import pallas as pl
from jax.sharding import PartitionSpec as P

epsilon = 1e-05
contract_cols = (((1,), (1,)), ((), ()))
contract_rows = (((0,), (0,)), ((), ()))


def local_terms(gate_sum, up_sum, back_sum, active_mask):
    sigmoid_gate = jax.nn.sigmoid(gate_sum)
    silu_gate = gate_sum * sigmoid_gate
    slope = sigmoid_gate * (1.0 + gate_sum * (1.0 - sigmoid_gate))
    hidden = (silu_gate * up_sum * active_mask).astype(jnp.bfloat16)
    gate_grad = (back_sum * up_sum * slope * active_mask).astype(jnp.bfloat16)
    up_grad = (back_sum * silu_gate * active_mask).astype(jnp.bfloat16)
    return (hidden, gate_grad, up_grad)


def back_kernel(grad_ref, weight_ref, out_ref):
    out_ref[...] = lax.dot_general(
        grad_ref[...], weight_ref[...], contract_cols, preferred_element_type=jnp.float32
    ).astype(out_ref.dtype)


def back_project(grad, weight):
    m, k = grad.shape
    n = weight.shape[0]
    tile = n // 4 if n % 512 == 0 else n
    return pl.pallas_call(
        back_kernel,
        grid=(n // tile,),
        in_specs=[
            pl.BlockSpec((m, k), lambda j: (0, 0)),
            pl.BlockSpec((tile, k), lambda j: (j, 0)),
        ],
        out_specs=pl.BlockSpec((m, tile), lambda j: (0, j)),
        out_shape=jax.ShapeDtypeStruct((m, n), jnp.bfloat16),
        cost_estimate=pl.CostEstimate(
            flops=2 * m * k * n, bytes_accessed=2 * (m * k + n * k + m * n), transcendentals=0
        ),
    )(grad, weight)


def per_device(inputs, norm_gain, w_gate, w_up, w_down, d_output, level_of_batch):
    groups = lax.axis_size("tensor")
    tensor_index = lax.axis_index("tensor")
    local_feat = w_gate.shape[0]
    local_cols = w_gate.shape[1]
    full_width = local_feat * lax.axis_size("dp")
    batches, local_rows, _ = inputs.shape
    wide_inputs = inputs.astype(jnp.float32)
    grad_all = lax.all_gather(d_output, "tensor", axis=1, tiled=True)
    rows = grad_all.shape[1]
    start = tensor_index * local_rows
    flat_grad = grad_all.reshape(rows * batches, local_feat)
    back_part = back_project(flat_grad, w_down)
    back_first = lax.psum(back_part, "dp")
    inputs_all, _ = lax.optimization_barrier((inputs, back_part))
    inputs_all = lax.all_gather(inputs_all, "tensor", axis=1, tiled=True).astype(jnp.float32)
    square_sum = jnp.sum(
        lax.all_gather(jnp.sum(inputs_all * inputs_all, axis=2), "dp", axis=0), axis=0
    )
    row_scale_all = lax.rsqrt(square_sum / full_width + epsilon)
    normed_all = (inputs_all * row_scale_all[:, :, None] * norm_gain).astype(jnp.bfloat16)
    row_scale = lax.dynamic_slice_in_dim(row_scale_all, start, local_rows, axis=1)

    flat_normed = normed_all.reshape(rows * batches, local_feat)
    halvings = 3 - level_of_batch
    active = (tensor_index < jnp.right_shift(groups, halvings)).astype(jnp.float32)
    active_mask = jnp.repeat(active, rows)[:, None]
    chunks = 1
    width = local_cols // chunks
    down_part = None
    normed_part = None
    hiddens, gate_grads, up_grads = [], [], []
    for chunk in range(chunks):
        cols = slice(chunk * width, (chunk + 1) * width)
        gate_w = w_gate[:, cols]
        up_w = w_up[:, cols]
        down_w = w_down[cols, :]
        gate_part = jnp.dot(flat_normed, gate_w, preferred_element_type=jnp.float32)
        up_part = jnp.dot(flat_normed, up_w, preferred_element_type=jnp.float32)
        parts = (gate_part.astype(jnp.bfloat16), up_part.astype(jnp.bfloat16))
        parts, back_sum = lax.optimization_barrier((parts, back_first))
        gate_sum, up_sum = lax.psum(parts, "dp")
        hidden, gate_grad, up_grad = local_terms(
            gate_sum.astype(jnp.float32),
            up_sum.astype(jnp.float32),
            back_sum.astype(jnp.float32),
            active_mask,
        )
        hiddens.append(hidden)
        gate_grads.append(gate_grad)
        up_grads.append(up_grad)
        down_term = jnp.dot(hidden, down_w, preferred_element_type=jnp.float32)
        normed_term = lax.dot_general(
            gate_grad, gate_w, contract_cols, preferred_element_type=jnp.float32
        ) + lax.dot_general(up_grad, up_w, contract_cols, preferred_element_type=jnp.float32)
        down_part = down_term if down_part is None else down_part + down_term
        normed_part = normed_term if normed_part is None else normed_part + normed_term
    hidden = jnp.concatenate(hiddens, axis=1)
    gate_grad = jnp.concatenate(gate_grads, axis=1)
    up_grad = jnp.concatenate(up_grads, axis=1)

    stacked = jnp.concatenate(
        [down_part.astype(jnp.bfloat16), normed_part.astype(jnp.bfloat16)], axis=1
    ).reshape(batches, rows, 2 * local_feat)
    stacked = stacked.transpose(1, 0, 2).reshape(rows, 2 * batches, local_feat)
    scaled_all = (inputs_all * row_scale_all[:, :, None]).reshape(rows * batches, local_feat)
    gain_part = jnp.sum(normed_part * scaled_all, axis=0)
    row_all = jnp.sum(
        normed_part * (norm_gain * inputs_all.reshape(rows * batches, local_feat)), axis=1
    )
    gathered = lax.all_gather(
        jnp.concatenate([gain_part, row_all]), ("dp", "tensor"), axis=0
    ).reshape(lax.axis_size("dp"), groups, -1)
    own = lax.dynamic_index_in_dim(gathered, lax.axis_index("dp"), 0, keepdims=False)
    d_gain = jnp.sum(own[:, :local_feat], axis=0)
    row_all = jnp.sum(gathered[:, :, local_feat:], axis=(0, 1)).reshape(batches, rows)
    row_product = lax.dynamic_slice_in_dim(row_all, start, local_rows, axis=1)
    hidden, flat_grad, _ = lax.optimization_barrier((hidden, flat_grad, stacked))
    shares = lax.psum_scatter(stacked, "tensor", scatter_dimension=0, tiled=True).astype(
        jnp.float32
    )
    shares = shares.reshape(local_rows, batches, 2, local_feat)
    down_output = shares[:, :, 0].transpose(1, 0, 2)
    normed_grad = shares[:, :, 1].transpose(1, 0, 2)

    down_out = lax.dot_general(
        hidden, flat_grad, contract_rows, preferred_element_type=jnp.float32
    ).astype(jnp.bfloat16)
    gate_out = lax.dot_general(
        flat_normed, gate_grad, contract_rows, preferred_element_type=jnp.float32
    ).astype(jnp.bfloat16)
    up_out = lax.dot_general(
        flat_normed, up_grad, contract_rows, preferred_element_type=jnp.float32
    ).astype(jnp.bfloat16)

    wide_grad = d_output.astype(jnp.float32)
    weighted = norm_gain * normed_grad
    outputs = (wide_inputs + down_output).astype(jnp.bfloat16)
    scale_cube = row_scale * row_scale * row_scale
    d_inputs = (
        wide_grad
        + row_scale[:, :, None] * weighted
        - wide_inputs * (scale_cube * row_product / full_width)[:, :, None]
    ).astype(jnp.bfloat16)
    return (outputs, d_inputs, d_gain, gate_out, up_out, down_out, row_product)


def solution(mesh):
    in_specs = (
        P(None, "tensor", "dp"),
        P("dp"),
        P("dp", "tensor"),
        P("dp", "tensor"),
        P("tensor", "dp"),
        P(None, "tensor", "dp"),
        P(),
    )
    out_specs = (
        P(None, "tensor", "dp"),
        P(None, "tensor", "dp"),
        P("dp"),
        P("dp", "tensor"),
        P("dp", "tensor"),
        P("tensor", "dp"),
        P(None, "tensor"),
    )
    return jax.shard_map(
        per_device, mesh=mesh, in_specs=in_specs, out_specs=out_specs, check_vma=False
    )
```

```python
import jax
import jax.numpy as jnp
from jax import lax
from jax.experimental import pallas as pl
from jax.sharding import PartitionSpec as P

epsilon = 1e-05
contract_cols = (((1,), (1,)), ((), ()))
contract_rows = (((0,), (0,)), ((), ()))


def local_terms(gate_sum, up_sum, back_sum, active_mask):
    sigmoid_gate = jax.nn.sigmoid(gate_sum)
    silu_gate = gate_sum * sigmoid_gate
    slope = sigmoid_gate * (1.0 + gate_sum * (1.0 - sigmoid_gate))
    hidden = (silu_gate * up_sum * active_mask).astype(jnp.bfloat16)
    gate_grad = (back_sum * up_sum * slope * active_mask).astype(jnp.bfloat16)
    up_grad = (back_sum * silu_gate * active_mask).astype(jnp.bfloat16)
    return (hidden, gate_grad, up_grad)


def back_kernel(grad_ref, weight_ref, out_ref):
    out_ref[...] = lax.dot_general(
        grad_ref[...], weight_ref[...], contract_cols, preferred_element_type=jnp.float32
    ).astype(out_ref.dtype)


def back_project(grad, weight):
    m, k = grad.shape
    n = weight.shape[0]
    tile = n // 4 if n % 512 == 0 else n
    return pl.pallas_call(
        back_kernel,
        grid=(n // tile,),
        in_specs=[
            pl.BlockSpec((m, k), lambda j: (0, 0)),
            pl.BlockSpec((tile, k), lambda j: (j, 0)),
        ],
        out_specs=pl.BlockSpec((m, tile), lambda j: (0, j)),
        out_shape=jax.ShapeDtypeStruct((m, n), jnp.bfloat16),
        cost_estimate=pl.CostEstimate(
            flops=2 * m * k * n, bytes_accessed=2 * (m * k + n * k + m * n), transcendentals=0
        ),
    )(grad, weight)


def per_device(inputs, norm_gain, w_gate, w_up, w_down, d_output, level_of_batch):
    groups = lax.axis_size("tensor")
    tensor_index = lax.axis_index("tensor")
    local_feat = w_gate.shape[0]
    local_cols = w_gate.shape[1]
    full_width = local_feat * lax.axis_size("dp")
    batches, local_rows, _ = inputs.shape
    wide_inputs = inputs.astype(jnp.float32)
    grad_all = lax.all_gather(d_output, "tensor", axis=1, tiled=True)
    rows = grad_all.shape[1]
    start = tensor_index * local_rows
    flat_grad = grad_all.reshape(rows * batches, local_feat)
    back_part = back_project(flat_grad, w_down)
    back_first = lax.psum(back_part, "dp")
    inputs_all, _ = lax.optimization_barrier((inputs, back_part))
    inputs_all = lax.all_gather(inputs_all, "tensor", axis=1, tiled=True).astype(jnp.float32)
    square_sum = jnp.sum(
        lax.all_gather(jnp.sum(inputs_all * inputs_all, axis=2), "dp", axis=0), axis=0
    )
    row_scale_all = lax.rsqrt(square_sum / full_width + epsilon)
    normed_all = (inputs_all * row_scale_all[:, :, None] * norm_gain).astype(jnp.bfloat16)
    row_scale = lax.dynamic_slice_in_dim(row_scale_all, start, local_rows, axis=1)

    flat_normed = normed_all.reshape(rows * batches, local_feat)
    halvings = 3 - level_of_batch
    active = (tensor_index < jnp.right_shift(groups, halvings)).astype(jnp.float32)
    active_mask = jnp.repeat(active, rows)[:, None]
    chunks = 1
    width = local_cols // chunks
    down_part = None
    normed_part = None
    hiddens, gate_grads, up_grads = [], [], []
    for chunk in range(chunks):
        cols = slice(chunk * width, (chunk + 1) * width)
        gate_w = w_gate[:, cols]
        up_w = w_up[:, cols]
        down_w = w_down[cols, :]
        gate_part = jnp.dot(flat_normed, gate_w, preferred_element_type=jnp.float32)
        up_part = jnp.dot(flat_normed, up_w, preferred_element_type=jnp.float32)
        parts = (gate_part.astype(jnp.bfloat16), up_part.astype(jnp.bfloat16))
        parts, back_sum = lax.optimization_barrier((parts, back_first))
        gate_sum, up_sum = lax.psum(parts, "dp")
        hidden, gate_grad, up_grad = local_terms(
            gate_sum.astype(jnp.float32),
            up_sum.astype(jnp.float32),
            back_sum.astype(jnp.float32),
            active_mask,
        )
        hiddens.append(hidden)
        gate_grads.append(gate_grad)
        up_grads.append(up_grad)
        down_term = jnp.dot(hidden, down_w, preferred_element_type=jnp.float32)
        normed_term = lax.dot_general(
            gate_grad, gate_w, contract_cols, preferred_element_type=jnp.float32
        ) + lax.dot_general(up_grad, up_w, contract_cols, preferred_element_type=jnp.float32)
        down_part = down_term if down_part is None else down_part + down_term
        normed_part = normed_term if normed_part is None else normed_part + normed_term
    hidden = jnp.concatenate(hiddens, axis=1)
    gate_grad = jnp.concatenate(gate_grads, axis=1)
    up_grad = jnp.concatenate(up_grads, axis=1)

    stacked = jnp.concatenate(
        [down_part.astype(jnp.bfloat16), normed_part.astype(jnp.bfloat16)], axis=1
    ).reshape(batches, rows, 2 * local_feat)
    stacked = stacked.transpose(1, 0, 2).reshape(rows, 2 * batches, local_feat)
    scaled_all = (inputs_all * row_scale_all[:, :, None]).reshape(rows * batches, local_feat)
    gain_part = jnp.sum(normed_part * scaled_all, axis=0)
    row_all = jnp.sum(
        normed_part * (norm_gain * inputs_all.reshape(rows * batches, local_feat)), axis=1
    )
    reduced = jnp.sum(
        lax.all_gather(jnp.concatenate([gain_part, row_all]), "tensor", axis=0), axis=0
    )
    d_gain = reduced[:local_feat]
    row_all = jnp.sum(lax.all_gather(reduced[local_feat:], "dp", axis=0), axis=0)
    row_all = row_all.reshape(batches, rows)
    row_product = lax.dynamic_slice_in_dim(row_all, start, local_rows, axis=1)
    shares = lax.psum_scatter(stacked, "tensor", scatter_dimension=0, tiled=True).astype(
        jnp.float32
    )
    shares = shares.reshape(local_rows, batches, 2, local_feat)
    down_output = shares[:, :, 0].transpose(1, 0, 2)
    normed_grad = shares[:, :, 1].transpose(1, 0, 2)

    down_out = lax.dot_general(
        hidden, flat_grad, contract_rows, preferred_element_type=jnp.float32
    ).astype(jnp.bfloat16)
    gate_out = lax.dot_general(
        flat_normed, gate_grad, contract_rows, preferred_element_type=jnp.float32
    ).astype(jnp.bfloat16)
    up_out = lax.dot_general(
        flat_normed, up_grad, contract_rows, preferred_element_type=jnp.float32
    ).astype(jnp.bfloat16)

    wide_grad = d_output.astype(jnp.float32)
    weighted = norm_gain * normed_grad
    outputs = (wide_inputs + down_output).astype(jnp.bfloat16)
    scale_cube = row_scale * row_scale * row_scale
    d_inputs = (
        wide_grad
        + row_scale[:, :, None] * weighted
        - wide_inputs * (scale_cube * row_product / full_width)[:, :, None]
    ).astype(jnp.bfloat16)
    return (outputs, d_inputs, d_gain, gate_out, up_out, down_out, row_product)


def solution(mesh):
    in_specs = (
        P(None, "tensor", "dp"),
        P("dp"),
        P("dp", "tensor"),
        P("dp", "tensor"),
        P("tensor", "dp"),
        P(None, "tensor", "dp"),
        P(),
    )
    out_specs = (
        P(None, "tensor", "dp"),
        P(None, "tensor", "dp"),
        P("dp"),
        P("dp", "tensor"),
        P("dp", "tensor"),
        P("tensor", "dp"),
        P(None, "tensor"),
    )
    return jax.shard_map(
        per_device, mesh=mesh, in_specs=in_specs, out_specs=out_specs, check_vma=False
    )
```
